32 devices in a mesh: lon: 16 (over z, y, core), lat: 2 (over x).
Axes of the slice: x: 2, y: 2, z: 4, core: 2. Of those that a mesh axis runs over, the one named last changes fastest.
Arguments:
- field: float32 [2, 512, 512], P(None, 'lon', 'lat'), may hold values from -6 to 6
- offsets: int32 [512], P('lat'), may hold values from 0 to 511, as said below
- fraction: float32 [512], P('lat'), may hold values from 0 to 1
- helm: float32 [2], replicated, may hold values from 4 to 32
Outputs:
- solution: float32 [2, 512, 512], P(None, 'lon', 'lat')
The draws below stay inside these ranges and needn't reach their ends.
Inputs may be any that keep to these rules, and one draw needn't show every extreme that they name: `offsets`: each row's offset is a whole number of longitude points; some row needs the whole circle but one point, some row none.
All inputs are finite; a program needn't handle non-finite values.
Results may differ from the reference program's by a relative error of at most 0.00002.
Values sent between devices are 32-bit elements; how exact they have to be, the bound alone decides.
No kernel may reach another device: no remote copies, remote signals or barrier semaphores. Data moves between devices by JAX's collectives and lax.ppermute only.
A program may use at most 64 MiB of HBM per device.

```python
import math
import jax
import jax.numpy as jnp
from jax import lax

LEV = 2
LON_DEV = 32
SMOOTH = 2
COARSE = 4
NLON = 512
NLAT = 512


def draw_offsets(key, part):
    first, second = jax.random.split(jax.random.fold_in(key, 17))
    remain = jax.random.randint(first, (NLAT,), 0, LON_DEV)
    blocks = jax.random.randint(second, (NLAT,), 0, NLON // LON_DEV)
    row = jnp.arange(NLAT)
    polar = (row < NLAT // 6) | (row >= NLAT - NLAT // 6)
    offset = remain + jnp.where(polar, blocks * LON_DEV, 0)
    offset = offset.at[0].set(NLON - 1)
    offset = offset.at[NLAT // 2].set(0)
    return offset.astype(jnp.int32)


def draw_field(key, part):
    keys = jax.random.split(jax.random.fold_in(key, 29), 5)
    lon = jnp.arange(NLON, dtype=jnp.float32)[None, :, None] / NLON
    lat = (jnp.arange(NLAT, dtype=jnp.float32)[None, None, :] + 0.5) / NLAT
    wave_lon = jax.random.randint(keys[0], (LEV, 1, 1), 1, 4).astype(jnp.float32)
    wave_lat = jax.random.randint(keys[1], (LEV, 1, 1), 1, 4).astype(jnp.float32)
    phase_lon = jax.random.uniform(keys[2], (LEV, 1, 1), jnp.float32, 0.0, 2.0 * math.pi)
    phase_lat = jax.random.uniform(keys[3], (LEV, 1, 1), jnp.float32, 0.0, 2.0 * math.pi)
    zonal = jnp.cos(2.0 * math.pi * wave_lon * lon + phase_lon)
    meridional = jnp.cos(math.pi * wave_lat * lat + phase_lat)
    noise = jnp.clip(jax.random.normal(keys[4], (LEV, NLON, NLAT), jnp.float32), -3.0, 3.0)
    values = 1.5 * zonal + 1.5 * meridional + noise
    return values.astype(jnp.float32)


def level_of(stream_key, dims, shards, smallest, top_value):
    gain = 1.0
    for dim, shards_of in shards:
        heights = jax.random.uniform(jax.random.fold_in(jax.random.fold_in(stream_key, 6), dim), (shards_of,), jnp.float32, smallest / len(shards), top_value / len(shards))
        gain = gain * jnp.repeat(jnp.exp(heights), dims[dim] // shards_of).reshape((-1,) + (1,) * (len(dims) - 1 - dim))
    return gain


def setup_inputs(seed: int = 0) -> dict:
    streams_of = jax.random.split(jax.random.key(seed), 5)
    field = draw_field(jax.random.fold_in(streams_of[4], 71), 0)
    offsets = draw_offsets(jax.random.fold_in(streams_of[4], 71), 0)
    fraction = jnp.clip(1.0 * jax.random.uniform(streams_of[2], (NLAT,), jnp.float32) ** level_of(streams_of[2], (NLAT,), ((0, 2),), -0.2, 0.2), 0.0, 1.0)
    helm = jnp.clip(jnp.exp(jax.random.uniform(streams_of[3], (LEV,), jnp.float32, math.log(4.0), math.log(32.0))), 4.0, 32.0)
    return dict(field=field, offsets=offsets, fraction=fraction, helm=helm)


OMEGA = 0.8


def pair_sum(x):
    zonal = jnp.roll(x, 1, axis=1) + jnp.roll(x, -1, axis=1)
    padded = jnp.pad(x, ((0, 0), (0, 0), (1, 1)))
    return zonal + padded[:, :, 2:] + padded[:, :, :-2]


def relax(x, rhs, coef):
    diag = 1.0 + 4.0 * coef
    applied = diag * x - coef * pair_sum(x)
    return x + OMEGA * (rhs - applied) / diag


def defect(x, rhs, coef):
    diag = 1.0 + 4.0 * coef
    return rhs - (diag * x - coef * pair_sum(x))


def restrict(x):
    lev, nlon, nlat = x.shape
    return x.reshape(lev, nlon // 2, 2, nlat // 2, 2).mean(axis=(2, 4))


def prolong(x):
    return jnp.repeat(jnp.repeat(x, 2, axis=1), 2, axis=2)


def reference(field, offsets, fraction, helm):
    column = jnp.arange(NLON, dtype=jnp.int32)
    index = ((column[:, None] - offsets[None, :]) % NLON).astype(jnp.int32)
    shifted = lax.map(lambda level: jnp.take_along_axis(level, index, axis=0), field)
    s = fraction[None, None, :]
    w_one = -s * (s - 1.0) * (s - 2.0) / 6.0
    w_two = (s + 1.0) * (s - 1.0) * (s - 2.0) / 2.0
    w_three = -(s + 1.0) * s * (s - 2.0) / 2.0
    w_four = (s + 1.0) * s * (s - 1.0) / 6.0
    departure = (w_one * jnp.roll(shifted, -1, axis=1) + w_two * shifted
                 + w_three * jnp.roll(shifted, 1, axis=1) + w_four * jnp.roll(shifted, 2, axis=1))
    coef0 = helm[:, None, None]
    coef1 = coef0 / 4.0
    coef2 = coef0 / 16.0
    level0 = jnp.zeros_like(departure)
    for sweep in range(SMOOTH):
        level0 = relax(level0, departure, coef0)
    rhs1 = restrict(defect(level0, departure, coef0))
    level1 = jnp.zeros_like(rhs1)
    for sweep in range(SMOOTH):
        level1 = relax(level1, rhs1, coef1)
    rhs2 = restrict(defect(level1, rhs1, coef1))
    level2 = jnp.zeros_like(rhs2)
    for sweep in range(COARSE):
        level2 = relax(level2, rhs2, coef2)
    level1 = level1 + prolong(level2)
    for sweep in range(SMOOTH):
        level1 = relax(level1, rhs1, coef1)
    level0 = level0 + prolong(level1)
    for sweep in range(SMOOTH):
        level0 = relax(level0, departure, coef0)
    return level0
```

```python
import jax
import jax.numpy as jnp
from jax import lax
from jax.sharding import PartitionSpec as P

SMOOTH = 2
COARSE = 4
OMEGA = 0.8

LAT_HALO = 64
LON_HALO = 32


def pair_sum(x):
    zonal = jnp.roll(x, 1, axis=1) + jnp.roll(x, -1, axis=1)
    return zonal + jnp.roll(x, -1, axis=2) + jnp.roll(x, 1, axis=2)


def relax(x, rhs, coef, valid):
    diag = 1.0 + 4.0 * coef
    applied = diag * x - coef * pair_sum(x)
    x = x + OMEGA * (rhs - applied) / diag
    return jnp.where(valid, x, 0.0)


def defect(x, rhs, coef):
    diag = 1.0 + 4.0 * coef
    return rhs - (diag * x - coef * pair_sum(x))


def restrict(x):
    lev, nlon, nlat = x.shape
    return x.reshape(lev, nlon // 2, 2, nlat // 2, 2).mean(axis=(2, 4))


def prolong(x):
    return jnp.repeat(jnp.repeat(x, 2, axis=1), 2, axis=2)


def lat_rows_valid(first, count, nlat):
    rows = first + jnp.arange(count, dtype=jnp.int32)
    return ((rows >= 0) & (rows < nlat))[None, None, :]


def per_device(field, offsets, fraction, helm):
    lev, width, rows = field.shape
    n_lon = lax.axis_size("lon")
    n_lat = lax.axis_size("lat")
    nlon = width * n_lon
    nlat = rows * n_lat
    d = lax.axis_index("lon")
    l = lax.axis_index("lat")
    hh = LAT_HALO
    hl = LON_HALO

    pack = jnp.concatenate(
        [
            field.reshape(lev * width, rows),
            offsets.astype(jnp.float32)[None, :],
            fraction[None, :],
        ],
        axis=0,
    )
    below = lax.ppermute(pack[:, rows - hh :], "lat", [(i, i + 1) for i in range(n_lat - 1)])
    above = lax.ppermute(pack[:, :hh], "lat", [(i + 1, i) for i in range(n_lat - 1)])
    ext = jnp.concatenate([below, pack, above], axis=1)
    erows = rows + 2 * hh
    fld = ext[: lev * width].reshape(lev, width, erows)
    off_e = ext[lev * width].astype(jnp.int32)
    frac_e = ext[lev * width + 1]

    full = lax.all_gather(fld, "lon", axis=1, tiled=True)

    w0 = width + 2 * hl
    span = w0 + 16
    s0 = d * width - hl - 8
    amt = (off_e - s0) % nlon
    nbits = (nlon - 1).bit_length()
    top = 1 << (nbits - 1)
    take = (amt // top % 2 == 1)[None, None, :]
    y = jnp.where(take, jnp.roll(full, top, axis=1), full)
    need = top - 1
    y = jnp.concatenate([y[:, nlon - need :], y[:, :span]], axis=1) if need else y[:, :span]
    for bit in range(nbits - 2, -1, -1):
        b = 1 << bit
        take = (amt // b % 2 == 1)[None, None, :]
        lo = b
        y = jnp.where(take, y[:, : y.shape[1] - b], y[:, b:])
    win = y

    s = frac_e[None, None, :]
    w_one = -s * (s - 1.0) * (s - 2.0) / 6.0
    w_two = (s + 1.0) * (s - 1.0) * (s - 2.0) / 2.0
    w_three = -(s + 1.0) * s * (s - 2.0) / 2.0
    w_four = (s + 1.0) * s * (s - 1.0) / 6.0
    departure = (
        w_one * win[:, 9 : 9 + w0]
        + w_two * win[:, 8 : 8 + w0]
        + w_three * win[:, 7 : 7 + w0]
        + w_four * win[:, 6 : 6 + w0]
    )

    first = l * rows - hh
    valid0 = lat_rows_valid(first, erows, nlat)
    valid1 = lat_rows_valid(first // 2, erows // 2, nlat // 2)
    valid2 = lat_rows_valid(first // 4, erows // 4, nlat // 4)

    coef0 = helm[:, None, None]
    coef1 = coef0 / 4.0
    coef2 = coef0 / 16.0
    level0 = jnp.zeros_like(departure)
    for sweep in range(SMOOTH):
        level0 = relax(level0, departure, coef0, valid0)
    rhs1 = restrict(defect(level0, departure, coef0))
    level1 = jnp.zeros_like(rhs1)
    for sweep in range(SMOOTH):
        level1 = relax(level1, rhs1, coef1, valid1)
    rhs2 = restrict(defect(level1, rhs1, coef1))
    level2 = jnp.zeros_like(rhs2)
    for sweep in range(COARSE):
        level2 = relax(level2, rhs2, coef2, valid2)
    level1 = level1 + prolong(level2)
    for sweep in range(SMOOTH):
        level1 = relax(level1, rhs1, coef1, valid1)
    level0 = level0 + prolong(level1)
    for sweep in range(SMOOTH):
        level0 = relax(level0, departure, coef0, valid0)
    return level0[:, hl : hl + width, hh : hh + rows]


def solution(mesh):
    return jax.shard_map(
        per_device,
        mesh=mesh,
        in_specs=(P(None, "lon", "lat"), P("lat"), P("lat"), P()),
        out_specs=P(None, "lon", "lat"),
        check_vma=False,
    )
```

```python
import functools

import jax
import jax.numpy as jnp
from jax import lax
from jax.experimental import pallas as pl
from jax.experimental.pallas import tpu as pltpu
from jax.sharding import PartitionSpec as P

SMOOTH = 2
COARSE = 4
OMEGA = 0.8

LAT_HALO = 64
LON_HALO = 32


def vcycle_kernel(helm_ref, valid_ref, rhs_ref, out_ref, *, wlon):
    rows, cols = rhs_ref.shape
    b0 = rhs_ref[...]
    valid = valid_ref[...] > 0.5
    row = lax.broadcasted_iota(jnp.int32, (rows, cols), 0)
    col = lax.broadcasted_iota(jnp.int32, (rows, cols), 1)
    coef0 = jnp.where(row < wlon, helm_ref[0], helm_ref[1])

    def shift(x, by, axis):
        n = x.shape[axis]
        return pltpu.roll(x, by % n, axis)

    def pair_sum(x, step):
        zonal = shift(x, step, 0) + shift(x, -step, 0)
        return zonal + shift(x, -step, 1) + shift(x, step, 1)

    def relax(x, rhs, coef, diag, step):
        if x is None:
            x = OMEGA * rhs / diag
        else:
            applied = diag * x - coef * pair_sum(x, step)
            x = x + OMEGA * (rhs - applied) / diag
        return jnp.where(valid, x, 0.0)

    def defect(x, rhs, coef, diag, step):
        return rhs - (diag * x - coef * pair_sum(x, step))

    def restrict(x, step):
        lon_pair = x + shift(x, -step, 0)
        return (lon_pair + shift(lon_pair, -step, 1)) * 0.25

    def prolong(x, step):
        x = jnp.where(row % (2 * step) == step, shift(x, step, 0), x)
        return jnp.where(col % (2 * step) == step, shift(x, step, 1), x)

    coef1 = coef0 / 4.0
    coef2 = coef0 / 16.0
    diag0 = 1.0 + 4.0 * coef0
    diag1 = 1.0 + 4.0 * coef1
    diag2 = 1.0 + 4.0 * coef2

    x0 = None
    for sweep in range(SMOOTH):
        x0 = relax(x0, b0, coef0, diag0, 1)
    b1 = restrict(defect(x0, b0, coef0, diag0, 1), 1)
    x1 = None
    for sweep in range(SMOOTH):
        x1 = relax(x1, b1, coef1, diag1, 2)
    b2 = restrict(defect(x1, b1, coef1, diag1, 2), 2)
    x2 = None
    for sweep in range(COARSE):
        x2 = relax(x2, b2, coef2, diag2, 4)
    x1 = x1 + prolong(x2, 2)
    for sweep in range(SMOOTH):
        x1 = relax(x1, b1, coef1, diag1, 2)
    x0 = x0 + prolong(x1, 1)
    for sweep in range(SMOOTH):
        x0 = relax(x0, b0, coef0, diag0, 1)
    out_ref[...] = x0


def vcycle(helm, valid, rhs, wlon):
    return pl.pallas_call(
        functools.partial(vcycle_kernel, wlon=wlon),
        out_shape=jax.ShapeDtypeStruct(rhs.shape, rhs.dtype),
        in_specs=[
            pl.BlockSpec(memory_space=pltpu.SMEM),
            pl.BlockSpec(memory_space=pltpu.VMEM),
            pl.BlockSpec(memory_space=pltpu.VMEM),
        ],
        out_specs=pl.BlockSpec(memory_space=pltpu.VMEM),
        name="vcycle",
    )(helm, valid, rhs)


def per_device(field, offsets, fraction, helm):
    lev, width, rows = field.shape
    n_lon = lax.axis_size("lon")
    n_lat = lax.axis_size("lat")
    nlon = width * n_lon
    nlat = rows * n_lat
    d = lax.axis_index("lon")
    l = lax.axis_index("lat")
    hh = LAT_HALO
    hl = LON_HALO

    full = lax.all_gather(field, "lon", axis=1, tiled=True)

    w0 = width + 2 * hl
    span = w0 + 16
    s0 = d * width - hl - 8
    amt = (offsets - s0) % nlon
    nbits = (nlon - 1).bit_length()
    top = 1 << (nbits - 1)
    take = (amt // top % 2 == 1)[None, None, :]
    y = jnp.where(take, jnp.roll(full, top, axis=1), full)
    need = top - 1
    y = jnp.concatenate([y[:, nlon - need :], y[:, :span]], axis=1) if need else y[:, :span]
    for bit in range(nbits - 2, -1, -1):
        b = 1 << bit
        take = (amt // b % 2 == 1)[None, None, :]
        y = jnp.where(take, y[:, : y.shape[1] - b], y[:, b:])
    win = y

    s = fraction[None, None, :]
    w_one = -s * (s - 1.0) * (s - 2.0) / 6.0
    w_two = (s + 1.0) * (s - 1.0) * (s - 2.0) / 2.0
    w_three = -(s + 1.0) * s * (s - 2.0) / 2.0
    w_four = (s + 1.0) * s * (s - 1.0) / 6.0
    departure = (
        w_one * win[:, 9 : 9 + w0]
        + w_two * win[:, 8 : 8 + w0]
        + w_three * win[:, 7 : 7 + w0]
        + w_four * win[:, 6 : 6 + w0]
    )

    below = lax.ppermute(departure[:, :, rows - hh :], "lat", [(i, i + 1) for i in range(n_lat - 1)])
    above = lax.ppermute(departure[:, :, :hh], "lat", [(i + 1, i) for i in range(n_lat - 1)])
    ext = jnp.concatenate([below, departure, above], axis=2)
    erows = rows + 2 * hh

    first = l * rows - hh
    lat_rows = first + jnp.arange(erows, dtype=jnp.int32)
    valid = ((lat_rows >= 0) & (lat_rows < nlat)).astype(jnp.float32)[None, :]

    out = vcycle(helm, valid, ext.reshape(lev * w0, erows), w0)
    return out.reshape(lev, w0, erows)[:, hl : hl + width, hh : hh + rows]


def solution(mesh):
    return jax.shard_map(
        per_device,
        mesh=mesh,
        in_specs=(P(None, "lon", "lat"), P("lat"), P("lat"), P()),
        out_specs=P(None, "lon", "lat"),
        check_vma=False,
    )
```

```python
import functools

import jax
import jax.numpy as jnp
from jax import lax
from jax.experimental import pallas as pl
from jax.experimental.pallas import tpu as pltpu
from jax.sharding import PartitionSpec as P

SMOOTH = 2
COARSE = 4
OMEGA = 0.8

LAT_HALO = 64
LON_HALO = 32


def vcycle_kernel(helm_ref, valid_ref, rhs_ref, out_ref, *, wlon):
    rows, cols = rhs_ref.shape
    b0 = rhs_ref[...]
    valid = valid_ref[...] > 0.5
    row = lax.broadcasted_iota(jnp.int32, (rows, cols), 0)
    col = lax.broadcasted_iota(jnp.int32, (rows, cols), 1)
    coef0 = jnp.where(row < wlon, helm_ref[0], helm_ref[1])

    def shift(x, by, axis):
        n = x.shape[axis]
        return pltpu.roll(x, by % n, axis)

    def pair_sum(x, step):
        zonal = shift(x, step, 0) + shift(x, -step, 0)
        return zonal + shift(x, -step, 1) + shift(x, step, 1)

    def relax(x, rhs, coef, diag, step):
        if x is None:
            x = OMEGA * rhs / diag
        else:
            applied = diag * x - coef * pair_sum(x, step)
            x = x + OMEGA * (rhs - applied) / diag
        return jnp.where(valid, x, 0.0)

    def defect(x, rhs, coef, diag, step):
        return rhs - (diag * x - coef * pair_sum(x, step))

    def restrict(x, step):
        lon_pair = x + shift(x, -step, 0)
        return (lon_pair + shift(lon_pair, -step, 1)) * 0.25

    def prolong(x, step):
        x = jnp.where(row % (2 * step) == step, shift(x, step, 0), x)
        return jnp.where(col % (2 * step) == step, shift(x, step, 1), x)

    coef1 = coef0 / 4.0
    coef2 = coef0 / 16.0
    diag0 = 1.0 + 4.0 * coef0
    diag1 = 1.0 + 4.0 * coef1
    diag2 = 1.0 + 4.0 * coef2

    x0 = None
    for sweep in range(SMOOTH):
        x0 = relax(x0, b0, coef0, diag0, 1)
    b1 = restrict(defect(x0, b0, coef0, diag0, 1), 1)
    x1 = None
    for sweep in range(SMOOTH):
        x1 = relax(x1, b1, coef1, diag1, 2)
    b2 = restrict(defect(x1, b1, coef1, diag1, 2), 2)
    x2 = None
    for sweep in range(COARSE):
        x2 = relax(x2, b2, coef2, diag2, 4)
    x1 = x1 + prolong(x2, 2)
    for sweep in range(SMOOTH):
        x1 = relax(x1, b1, coef1, diag1, 2)
    x0 = x0 + prolong(x1, 1)
    for sweep in range(SMOOTH):
        x0 = relax(x0, b0, coef0, diag0, 1)
    out_ref[...] = x0


def vcycle(helm, valid, rhs, wlon):
    return pl.pallas_call(
        functools.partial(vcycle_kernel, wlon=wlon),
        out_shape=jax.ShapeDtypeStruct(rhs.shape, rhs.dtype),
        in_specs=[
            pl.BlockSpec(memory_space=pltpu.SMEM),
            pl.BlockSpec(memory_space=pltpu.VMEM),
            pl.BlockSpec(memory_space=pltpu.VMEM),
        ],
        out_specs=pl.BlockSpec(memory_space=pltpu.VMEM),
        name="vcycle",
    )(helm, valid, rhs)


def per_device(field, offsets, fraction, helm):
    lev, width, rows = field.shape
    n_lon = lax.axis_size("lon")
    n_lat = lax.axis_size("lat")
    nlon = width * n_lon
    nlat = rows * n_lat
    l = lax.axis_index("lat")
    hh = LAT_HALO
    hl = LON_HALO

    parts = [field] + [
        lax.ppermute(field, "lon", [(i, (i - k) % n_lon) for i in range(n_lon)])
        for k in range(1, n_lon)
    ]
    full = jnp.concatenate(parts, axis=1)

    w0 = width + 2 * hl
    span = w0 + 16
    amt = (offsets + hl + 8) % nlon
    nbits = (nlon - 1).bit_length()
    top = 1 << (nbits - 1)
    take = (amt // top % 2 == 1)[None, None, :]
    y = jnp.where(take, jnp.roll(full, top, axis=1), full)
    need = top - 1
    y = jnp.concatenate([y[:, nlon - need :], y[:, :span]], axis=1) if need else y[:, :span]
    for bit in range(nbits - 2, -1, -1):
        b = 1 << bit
        take = (amt // b % 2 == 1)[None, None, :]
        y = jnp.where(take, y[:, : y.shape[1] - b], y[:, b:])
    win = y

    s = fraction[None, None, :]
    w_one = -s * (s - 1.0) * (s - 2.0) / 6.0
    w_two = (s + 1.0) * (s - 1.0) * (s - 2.0) / 2.0
    w_three = -(s + 1.0) * s * (s - 2.0) / 2.0
    w_four = (s + 1.0) * s * (s - 1.0) / 6.0
    departure = (
        w_one * win[:, 9 : 9 + w0]
        + w_two * win[:, 8 : 8 + w0]
        + w_three * win[:, 7 : 7 + w0]
        + w_four * win[:, 6 : 6 + w0]
    )

    below = lax.ppermute(departure[:, :, rows - hh :], "lat", [(i, i + 1) for i in range(n_lat - 1)])
    above = lax.ppermute(departure[:, :, :hh], "lat", [(i + 1, i) for i in range(n_lat - 1)])
    ext = jnp.concatenate([below, departure, above], axis=2)
    erows = rows + 2 * hh

    first = l * rows - hh
    lat_rows = first + jnp.arange(erows, dtype=jnp.int32)
    valid = ((lat_rows >= 0) & (lat_rows < nlat)).astype(jnp.float32)[None, :]

    out = vcycle(helm, valid, ext.reshape(lev * w0, erows), w0)
    return out.reshape(lev, w0, erows)[:, hl : hl + width, hh : hh + rows]


def solution(mesh):
    return jax.shard_map(
        per_device,
        mesh=mesh,
        in_specs=(P(None, "lon", "lat"), P("lat"), P("lat"), P()),
        out_specs=P(None, "lon", "lat"),
        check_vma=False,
    )
```

```python
import functools

import jax
import jax.numpy as jnp
from jax import lax
from jax.experimental import pallas as pl
from jax.experimental.pallas import tpu as pltpu
from jax.sharding import PartitionSpec as P

SMOOTH = 2
COARSE = 4
OMEGA = 0.8


LAT_HALO = 64
LON_HALO = 32


def vcycle_kernel(helm_ref, valid_ref, rhs_ref, out_ref, *, wlon):
    rows, cols = rhs_ref.shape
    b0 = rhs_ref[...]
    valid = valid_ref[...] > 0.5
    row = lax.broadcasted_iota(jnp.int32, (rows, cols), 0)
    col = lax.broadcasted_iota(jnp.int32, (rows, cols), 1)
    coef0 = jnp.where(row < wlon, helm_ref[0], helm_ref[1])

    def shift(x, by, axis):
        n = x.shape[axis]
        return pltpu.roll(x, by % n, axis)

    def pair_sum(x, step):
        zonal = shift(x, step, 0) + shift(x, -step, 0)
        return zonal + shift(x, -step, 1) + shift(x, step, 1)

    def relax(x, rhs, coef, diag, step):
        if x is None:
            x = OMEGA * rhs / diag
        else:
            applied = diag * x - coef * pair_sum(x, step)
            x = x + OMEGA * (rhs - applied) / diag
        return jnp.where(valid, x, 0.0)

    def defect(x, rhs, coef, diag, step):
        return rhs - (diag * x - coef * pair_sum(x, step))

    def restrict(x, step):
        lon_pair = x + shift(x, -step, 0)
        return (lon_pair + shift(lon_pair, -step, 1)) * 0.25

    def prolong(x, step):
        x = jnp.where(row % (2 * step) == step, shift(x, step, 0), x)
        return jnp.where(col % (2 * step) == step, shift(x, step, 1), x)

    coef1 = coef0 / 4.0
    coef2 = coef0 / 16.0
    diag0 = 1.0 + 4.0 * coef0
    diag1 = 1.0 + 4.0 * coef1
    diag2 = 1.0 + 4.0 * coef2

    x0 = None
    for sweep in range(SMOOTH):
        x0 = relax(x0, b0, coef0, diag0, 1)
    b1 = restrict(defect(x0, b0, coef0, diag0, 1), 1)
    x1 = None
    for sweep in range(SMOOTH):
        x1 = relax(x1, b1, coef1, diag1, 2)
    b2 = restrict(defect(x1, b1, coef1, diag1, 2), 2)
    x2 = None
    for sweep in range(COARSE):
        x2 = relax(x2, b2, coef2, diag2, 4)
    x1 = x1 + prolong(x2, 2)
    for sweep in range(SMOOTH):
        x1 = relax(x1, b1, coef1, diag1, 2)
    x0 = x0 + prolong(x1, 1)
    for sweep in range(SMOOTH):
        x0 = relax(x0, b0, coef0, diag0, 1)
    out_ref[...] = x0


def vcycle(helm, valid, rhs, wlon):
    return pl.pallas_call(
        functools.partial(vcycle_kernel, wlon=wlon),
        out_shape=jax.ShapeDtypeStruct(rhs.shape, rhs.dtype),
        in_specs=[
            pl.BlockSpec(memory_space=pltpu.SMEM),
            pl.BlockSpec(memory_space=pltpu.VMEM),
            pl.BlockSpec(memory_space=pltpu.VMEM),
        ],
        out_specs=pl.BlockSpec(memory_space=pltpu.VMEM),
        name="vcycle",
    )(helm, valid, rhs)


def per_device(field, offsets, fraction, helm):
    lev, width, rows = field.shape
    n_lon = lax.axis_size("lon")
    n_lat = lax.axis_size("lat")
    nlon = width * n_lon
    nlat = rows * n_lat
    l = lax.axis_index("lat")
    hh = LAT_HALO
    hl = LON_HALO

    pairs = n_lon // 2
    same = [field] + [
        lax.ppermute(field, "lon", [(i, (i - 2 * k) % n_lon) for i in range(n_lon)])
        for k in range(1, pairs)
    ]
    sibling = [(i, i ^ 1) for i in range(n_lon)]
    relay = lax.ppermute(jnp.concatenate(same[1:], axis=1), "lon", sibling)
    other = [lax.ppermute(field, "lon", sibling)] + jnp.split(relay, pairs - 1, axis=1)
    odd = (lax.axis_index("lon") % 2 == 1)
    blocks = []
    for k in range(pairs):
        blocks.append(jnp.where(odd, other[k], same[k]))
        blocks.append(jnp.where(odd, same[k], other[k]))
    full = jnp.concatenate(blocks, axis=1)

    w0 = width + 2 * hl
    span = w0 + 16
    amt = (offsets + hl + 8 - jnp.where(odd, width, 0)) % nlon
    nbits = (nlon - 1).bit_length()
    top = 1 << (nbits - 1)
    take = (amt // top % 2 == 1)[None, None, :]
    y = jnp.where(take, jnp.roll(full, top, axis=1), full)
    need = top - 1
    y = jnp.concatenate([y[:, nlon - need :], y[:, :span]], axis=1) if need else y[:, :span]
    for bit in range(nbits - 2, -1, -1):
        b = 1 << bit
        take = (amt // b % 2 == 1)[None, None, :]
        y = jnp.where(take, y[:, : y.shape[1] - b], y[:, b:])
    win = y

    s = fraction[None, None, :]
    w_one = -s * (s - 1.0) * (s - 2.0) / 6.0
    w_two = (s + 1.0) * (s - 1.0) * (s - 2.0) / 2.0
    w_three = -(s + 1.0) * s * (s - 2.0) / 2.0
    w_four = (s + 1.0) * s * (s - 1.0) / 6.0
    departure = (
        w_one * win[:, 9 : 9 + w0]
        + w_two * win[:, 8 : 8 + w0]
        + w_three * win[:, 7 : 7 + w0]
        + w_four * win[:, 6 : 6 + w0]
    )

    below = lax.ppermute(departure[:, :, rows - hh :], "lat", [(i, i + 1) for i in range(n_lat - 1)])
    above = lax.ppermute(departure[:, :, :hh], "lat", [(i + 1, i) for i in range(n_lat - 1)])
    ext = jnp.concatenate([below, departure, above], axis=2)
    erows = rows + 2 * hh

    first = l * rows - hh
    lat_rows = first + jnp.arange(erows, dtype=jnp.int32)
    valid = ((lat_rows >= 0) & (lat_rows < nlat)).astype(jnp.float32)[None, :]

    out = vcycle(helm, valid, ext.reshape(lev * w0, erows), w0)
    return out.reshape(lev, w0, erows)[:, hl : hl + width, hh : hh + rows]


def solution(mesh):
    return jax.shard_map(
        per_device,
        mesh=mesh,
        in_specs=(P(None, "lon", "lat"), P("lat"), P("lat"), P()),
        out_specs=P(None, "lon", "lat"),
        check_vma=False,
    )
```

```python
import functools

import jax
import jax.numpy as jnp
from jax import lax
from jax.experimental import pallas as pl
from jax.experimental.pallas import tpu as pltpu
from jax.sharding import PartitionSpec as P

SMOOTH = 2
COARSE = 4
OMEGA = 0.8


LAT_HALO = 64
LON_HALO = 32


def vcycle_kernel(helm_ref, valid_ref, rhs_ref, out_ref, *, wlon, width, hl, rows, hh):
    rows_total, cols = rhs_ref.shape
    b0 = rhs_ref[...]
    valid = valid_ref[...] > 0.5
    row = lax.broadcasted_iota(jnp.int32, (rows_total, cols), 0)
    col = lax.broadcasted_iota(jnp.int32, (rows_total, cols), 1)
    coef0 = jnp.where(row < wlon, helm_ref[0], helm_ref[1])

    def shift(x, by, axis):
        n = x.shape[axis]
        return pltpu.roll(x, by % n, axis)

    def pair_sum(x, step):
        zonal = shift(x, step, 0) + shift(x, -step, 0)
        return zonal + shift(x, -step, 1) + shift(x, step, 1)

    def relax(x, rhs, coef, diag, step):
        if x is None:
            x = OMEGA * rhs / diag
        else:
            applied = diag * x - coef * pair_sum(x, step)
            x = x + OMEGA * (rhs - applied) / diag
        return jnp.where(valid, x, 0.0)

    def defect(x, rhs, coef, diag, step):
        return rhs - (diag * x - coef * pair_sum(x, step))

    def restrict(x, step):
        lon_pair = x + shift(x, -step, 0)
        return (lon_pair + shift(lon_pair, -step, 1)) * 0.25

    def prolong(x, step):
        x = jnp.where(row % (2 * step) == step, shift(x, step, 0), x)
        return jnp.where(col % (2 * step) == step, shift(x, step, 1), x)

    coef1 = coef0 / 4.0
    coef2 = coef0 / 16.0
    diag0 = 1.0 + 4.0 * coef0
    diag1 = 1.0 + 4.0 * coef1
    diag2 = 1.0 + 4.0 * coef2

    x0 = None
    for sweep in range(SMOOTH):
        x0 = relax(x0, b0, coef0, diag0, 1)
    b1 = restrict(defect(x0, b0, coef0, diag0, 1), 1)
    x1 = None
    for sweep in range(SMOOTH):
        x1 = relax(x1, b1, coef1, diag1, 2)
    b2 = restrict(defect(x1, b1, coef1, diag1, 2), 2)
    x2 = None
    for sweep in range(COARSE):
        x2 = relax(x2, b2, coef2, diag2, 4)
    x1 = x1 + prolong(x2, 2)
    for sweep in range(SMOOTH):
        x1 = relax(x1, b1, coef1, diag1, 2)
    x0 = x0 + prolong(x1, 1)
    for sweep in range(SMOOTH):
        x0 = relax(x0, b0, coef0, diag0, 1)
    x0 = shift(x0, -hh, 1)[:, :rows]
    for k in range(rows_total // wlon):
        out_ref[k * width : (k + 1) * width, :] = x0[k * wlon + hl : k * wlon + hl + width, :]


def vcycle(helm, valid, rhs, wlon, width, hl, rows, hh):
    lev = rhs.shape[0] // wlon
    return pl.pallas_call(
        functools.partial(vcycle_kernel, wlon=wlon, width=width, hl=hl, rows=rows, hh=hh),
        out_shape=jax.ShapeDtypeStruct((lev * width, rows), rhs.dtype),
        in_specs=[
            pl.BlockSpec(memory_space=pltpu.SMEM),
            pl.BlockSpec(memory_space=pltpu.VMEM),
            pl.BlockSpec(memory_space=pltpu.VMEM),
        ],
        out_specs=pl.BlockSpec(memory_space=pltpu.VMEM),
        name="vcycle",
    )(helm, valid, rhs)


def per_device(field, offsets, fraction, helm):
    lev, width, rows = field.shape
    n_lon = lax.axis_size("lon")
    n_lat = lax.axis_size("lat")
    nlon = width * n_lon
    nlat = rows * n_lat
    l = lax.axis_index("lat")
    hh = LAT_HALO
    hl = LON_HALO

    pairs = n_lon // 2
    same = [field] + [
        lax.ppermute(field, "lon", [(i, (i - 2 * k) % n_lon) for i in range(n_lon)])
        for k in range(1, pairs)
    ]
    sibling = [(i, i ^ 1) for i in range(n_lon)]
    first_sib = lax.ppermute(field, "lon", sibling)
    edge = jnp.stack([offsets.astype(jnp.float32), fraction])
    up = [(i, i + 1) for i in range(n_lat - 1)]
    down = [(i + 1, i) for i in range(n_lat - 1)]
    edge_lo = lax.ppermute(edge[:, rows - hh :], "lat", up)
    edge_hi = lax.ppermute(edge[:, :hh], "lat", down)

    relay = lax.ppermute(jnp.concatenate(same[1:], axis=1), "lon", sibling)
    other = [first_sib] + jnp.split(relay, pairs - 1, axis=1)
    held = jnp.concatenate(same, axis=1)

    def to_lat(x, lat_pairs, core_of):
        return lax.ppermute(
            x,
            ("lon", "lat"),
            [(i * n_lat + a, core_of(i) * n_lat + b) for i in range(n_lon) for a, b in lat_pairs],
        )

    strip_top, strip_bottom = held[:, :, rows - hh :], held[:, :, :hh]
    lo_same = jnp.split(to_lat(strip_top, up, lambda i: i), pairs, axis=1)
    lo_other = jnp.split(to_lat(strip_top, up, lambda i: i ^ 1), pairs, axis=1)
    hi_same = jnp.split(to_lat(strip_bottom, down, lambda i: i), pairs, axis=1)
    hi_other = jnp.split(to_lat(strip_bottom, down, lambda i: i ^ 1), pairs, axis=1)
    same = [jnp.concatenate(z, axis=2) for z in zip(lo_same, same, hi_same)]
    other = [jnp.concatenate(z, axis=2) for z in zip(lo_other, other, hi_other)]
    odd = (lax.axis_index("lon") % 2 == 1)
    blocks = []
    for k in range(pairs):
        blocks.append(jnp.where(odd, other[k], same[k]))
        blocks.append(jnp.where(odd, same[k], other[k]))
    full = jnp.concatenate(blocks, axis=1)
    erows = rows + 2 * hh
    edge = jnp.concatenate([edge_lo, edge, edge_hi], axis=1)
    offsets = edge[0].astype(jnp.int32)
    fraction = edge[1]

    w0 = width + 2 * hl
    span = w0 + 16
    amt = (offsets + hl + 8 - jnp.where(odd, width, 0)) % nlon
    nbits = (nlon - 1).bit_length()
    top = 1 << (nbits - 1)
    take = (amt // top % 2 == 1)[None, None, :]
    y = jnp.where(take, jnp.roll(full, top, axis=1), full)
    need = top - 1
    y = jnp.concatenate([y[:, nlon - need :], y[:, :span]], axis=1) if need else y[:, :span]
    for bit in range(nbits - 2, -1, -1):
        b = 1 << bit
        take = (amt // b % 2 == 1)[None, None, :]
        y = jnp.where(take, y[:, : y.shape[1] - b], y[:, b:])
    win = y

    s = fraction[None, None, :]
    w_one = -s * (s - 1.0) * (s - 2.0) / 6.0
    w_two = (s + 1.0) * (s - 1.0) * (s - 2.0) / 2.0
    w_three = -(s + 1.0) * s * (s - 2.0) / 2.0
    w_four = (s + 1.0) * s * (s - 1.0) / 6.0
    departure = (
        w_one * win[:, 9 : 9 + w0]
        + w_two * win[:, 8 : 8 + w0]
        + w_three * win[:, 7 : 7 + w0]
        + w_four * win[:, 6 : 6 + w0]
    )

    first = l * rows - hh
    lat_rows = first + jnp.arange(erows, dtype=jnp.int32)
    valid = ((lat_rows >= 0) & (lat_rows < nlat)).astype(jnp.float32)[None, :]

    out = vcycle(helm, valid, departure.reshape(lev * w0, erows), w0, width, hl, rows, hh)
    return out.reshape(lev, width, rows)


def solution(mesh):
    return jax.shard_map(
        per_device,
        mesh=mesh,
        in_specs=(P(None, "lon", "lat"), P("lat"), P("lat"), P()),
        out_specs=P(None, "lon", "lat"),
        check_vma=False,
    )
```

```python
import functools

import jax
import jax.numpy as jnp
from jax import lax
from jax.experimental import pallas as pl
from jax.experimental.pallas import tpu as pltpu
from jax.sharding import PartitionSpec as P

SMOOTH = 2
COARSE = 4
OMEGA = 0.8


LAT_HALO = 64
LON_HALO = 32


def vcycle_kernel(helm_ref, valid_ref, rhs_ref, out_ref, *, wlon, width, hl, rows, hh):
    rows_total, cols = rhs_ref.shape
    b0 = rhs_ref[...]
    valid = valid_ref[...] > 0.5
    row = lax.broadcasted_iota(jnp.int32, (rows_total, cols), 0)
    col = lax.broadcasted_iota(jnp.int32, (rows_total, cols), 1)
    coef0 = jnp.where(row < wlon, helm_ref[0], helm_ref[1])

    def shift(x, by, axis):
        n = x.shape[axis]
        return pltpu.roll(x, by % n, axis)

    def pair_sum(x, step):
        zonal = shift(x, step, 0) + shift(x, -step, 0)
        return zonal + shift(x, -step, 1) + shift(x, step, 1)

    def relax(x, rhs, coef, diag, step):
        if x is None:
            x = OMEGA * rhs / diag
        else:
            applied = diag * x - coef * pair_sum(x, step)
            x = x + OMEGA * (rhs - applied) / diag
        return jnp.where(valid, x, 0.0)

    def defect(x, rhs, coef, diag, step):
        return rhs - (diag * x - coef * pair_sum(x, step))

    def restrict(x, step):
        lon_pair = x + shift(x, -step, 0)
        return (lon_pair + shift(lon_pair, -step, 1)) * 0.25

    def prolong(x, step):
        x = jnp.where(row % (2 * step) == step, shift(x, step, 0), x)
        return jnp.where(col % (2 * step) == step, shift(x, step, 1), x)

    coef1 = coef0 / 4.0
    coef2 = coef0 / 16.0
    diag0 = 1.0 + 4.0 * coef0
    diag1 = 1.0 + 4.0 * coef1
    diag2 = 1.0 + 4.0 * coef2

    x0 = None
    for sweep in range(SMOOTH):
        x0 = relax(x0, b0, coef0, diag0, 1)
    b1 = restrict(defect(x0, b0, coef0, diag0, 1), 1)
    x1 = None
    for sweep in range(SMOOTH):
        x1 = relax(x1, b1, coef1, diag1, 2)
    b2 = restrict(defect(x1, b1, coef1, diag1, 2), 2)
    x2 = None
    for sweep in range(COARSE):
        x2 = relax(x2, b2, coef2, diag2, 4)
    x1 = x1 + prolong(x2, 2)
    for sweep in range(SMOOTH):
        x1 = relax(x1, b1, coef1, diag1, 2)
    x0 = x0 + prolong(x1, 1)
    for sweep in range(SMOOTH):
        x0 = relax(x0, b0, coef0, diag0, 1)
    x0 = shift(x0, -hh, 1)[:, :rows]
    for k in range(rows_total // wlon):
        out_ref[k * width : (k + 1) * width, :] = x0[k * wlon + hl : k * wlon + hl + width, :]


def vcycle(helm, valid, rhs, wlon, width, hl, rows, hh):
    lev = rhs.shape[0] // wlon
    return pl.pallas_call(
        functools.partial(vcycle_kernel, wlon=wlon, width=width, hl=hl, rows=rows, hh=hh),
        out_shape=jax.ShapeDtypeStruct((lev * width, rows), rhs.dtype),
        in_specs=[
            pl.BlockSpec(memory_space=pltpu.SMEM),
            pl.BlockSpec(memory_space=pltpu.VMEM),
            pl.BlockSpec(memory_space=pltpu.VMEM),
        ],
        out_specs=pl.BlockSpec(memory_space=pltpu.VMEM),
        name="vcycle",
    )(helm, valid, rhs)


def per_device(field, offsets, fraction, helm):
    lev, width, rows = field.shape
    n_lon = lax.axis_size("lon")
    n_lat = lax.axis_size("lat")
    nlon = width * n_lon
    nlat = rows * n_lat
    l = lax.axis_index("lat")
    hh = LAT_HALO
    hl = LON_HALO

    pairs = n_lon // 2
    same = [field] + [
        lax.ppermute(field, "lon", [(i, (i - 2 * k) % n_lon) for i in range(n_lon)])
        for k in range(1, pairs)
    ]
    sibling = [(i, i ^ 1) for i in range(n_lon)]
    first_sib = lax.ppermute(field, "lon", sibling)
    ring = [(i, (i + 1) % n_lat) for i in range(n_lat)]
    hello = lax.ppermute(fraction[:8], "lat", ring)
    relay = lax.ppermute(jnp.concatenate(same[1:], axis=1), "lon", sibling)
    other = [first_sib] + jnp.split(relay, pairs - 1, axis=1)
    odd = (lax.axis_index("lon") % 2 == 1)
    blocks = []
    for k in range(pairs):
        blocks.append(jnp.where(odd, other[k], same[k]))
        blocks.append(jnp.where(odd, same[k], other[k]))
    full = jnp.concatenate(blocks, axis=1)

    w0 = width + 2 * hl
    span = w0 + 16
    amt = (offsets + hl + 8 - jnp.where(odd, width, 0)) % nlon
    nbits = (nlon - 1).bit_length()
    top = 1 << (nbits - 1)
    take = (amt // top % 2 == 1)[None, None, :]
    y = jnp.where(take, jnp.roll(full, top, axis=1), full)
    need = top - 1
    y = jnp.concatenate([y[:, nlon - need :], y[:, :span]], axis=1) if need else y[:, :span]
    for bit in range(nbits - 2, -1, -1):
        b = 1 << bit
        take = (amt // b % 2 == 1)[None, None, :]
        y = jnp.where(take, y[:, : y.shape[1] - b], y[:, b:])
    win = y

    s = fraction[None, None, :]
    w_one = -s * (s - 1.0) * (s - 2.0) / 6.0
    w_two = (s + 1.0) * (s - 1.0) * (s - 2.0) / 2.0
    w_three = -(s + 1.0) * s * (s - 2.0) / 2.0
    w_four = (s + 1.0) * s * (s - 1.0) / 6.0
    departure = (
        w_one * win[:, 9 : 9 + w0]
        + w_two * win[:, 8 : 8 + w0]
        + w_three * win[:, 7 : 7 + w0]
        + w_four * win[:, 6 : 6 + w0]
    )

    up = [(i, i + 1) for i in range(n_lat - 1)]
    down = [(i + 1, i) for i in range(n_lat - 1)]
    below = lax.ppermute(departure[:, :, rows - hh :], "lat", up)
    above = lax.ppermute(departure[:, :, :hh], "lat", down)
    departure = jnp.concatenate([below, departure, above], axis=2)
    erows = rows + 2 * hh

    first = l * rows - hh
    lat_rows = first + jnp.arange(erows, dtype=jnp.int32)
    valid = (lat_rows >= 0) & (lat_rows < nlat) & (hello[0] == hello[0])
    valid = valid.astype(jnp.float32)[None, :]

    out = vcycle(helm, valid, departure.reshape(lev * w0, erows), w0, width, hl, rows, hh)
    return out.reshape(lev, width, rows)


def solution(mesh):
    return jax.shard_map(
        per_device,
        mesh=mesh,
        in_specs=(P(None, "lon", "lat"), P("lat"), P("lat"), P()),
        out_specs=P(None, "lon", "lat"),
        check_vma=False,
    )
```

```python
import functools

import jax
import jax.numpy as jnp
from jax import lax
from jax.experimental import pallas as pl
from jax.experimental.pallas import tpu as pltpu
from jax.sharding import PartitionSpec as P

SMOOTH = 2
COARSE = 4
OMEGA = 0.8


LAT_HALO = 64
LON_HALO = 32


def vcycle_kernel(helm_ref, valid_ref, rhs_ref, halo_ref, out_ref, *, wlon, width, hl):
    rows_total, rows = rhs_ref.shape
    b0 = jnp.concatenate([rhs_ref[...], halo_ref[...]], axis=1)
    cols = b0.shape[1]
    valid = valid_ref[...] > 0.5
    row = lax.broadcasted_iota(jnp.int32, (rows_total, cols), 0)
    col = lax.broadcasted_iota(jnp.int32, (rows_total, cols), 1)
    coef0 = jnp.where(row < wlon, helm_ref[0], helm_ref[1])

    def shift(x, by, axis):
        n = x.shape[axis]
        return pltpu.roll(x, by % n, axis)

    def pair_sum(x, step):
        zonal = shift(x, step, 0) + shift(x, -step, 0)
        return zonal + shift(x, -step, 1) + shift(x, step, 1)

    def relax(x, rhs, coef, diag, step):
        if x is None:
            x = OMEGA * rhs / diag
        else:
            applied = diag * x - coef * pair_sum(x, step)
            x = x + OMEGA * (rhs - applied) / diag
        return jnp.where(valid, x, 0.0)

    def defect(x, rhs, coef, diag, step):
        return rhs - (diag * x - coef * pair_sum(x, step))

    def restrict(x, step):
        lon_pair = x + shift(x, -step, 0)
        return (lon_pair + shift(lon_pair, -step, 1)) * 0.25

    def prolong(x, step):
        x = jnp.where(row % (2 * step) == step, shift(x, step, 0), x)
        return jnp.where(col % (2 * step) == step, shift(x, step, 1), x)

    coef1 = coef0 / 4.0
    coef2 = coef0 / 16.0
    diag0 = 1.0 + 4.0 * coef0
    diag1 = 1.0 + 4.0 * coef1
    diag2 = 1.0 + 4.0 * coef2

    x0 = None
    for sweep in range(SMOOTH):
        x0 = relax(x0, b0, coef0, diag0, 1)
    b1 = restrict(defect(x0, b0, coef0, diag0, 1), 1)
    x1 = None
    for sweep in range(SMOOTH):
        x1 = relax(x1, b1, coef1, diag1, 2)
    b2 = restrict(defect(x1, b1, coef1, diag1, 2), 2)
    x2 = None
    for sweep in range(COARSE):
        x2 = relax(x2, b2, coef2, diag2, 4)
    x1 = x1 + prolong(x2, 2)
    for sweep in range(SMOOTH):
        x1 = relax(x1, b1, coef1, diag1, 2)
    x0 = x0 + prolong(x1, 1)
    for sweep in range(SMOOTH):
        x0 = relax(x0, b0, coef0, diag0, 1)
    x0 = x0[:, :rows]
    for k in range(rows_total // wlon):
        out_ref[k * width : (k + 1) * width, :] = x0[k * wlon + hl : k * wlon + hl + width, :]


def vcycle(helm, valid, rhs, halo, wlon, width, hl):
    lev = rhs.shape[0] // wlon
    return pl.pallas_call(
        functools.partial(vcycle_kernel, wlon=wlon, width=width, hl=hl),
        out_shape=jax.ShapeDtypeStruct((lev * width, rhs.shape[1]), rhs.dtype),
        in_specs=[
            pl.BlockSpec(memory_space=pltpu.SMEM),
            pl.BlockSpec(memory_space=pltpu.VMEM),
            pl.BlockSpec(memory_space=pltpu.VMEM),
            pl.BlockSpec(memory_space=pltpu.VMEM),
        ],
        out_specs=pl.BlockSpec(memory_space=pltpu.VMEM),
        name="vcycle",
    )(helm, valid, rhs, halo)


def per_device(field, offsets, fraction, helm):
    lev, width, rows = field.shape
    n_lon = lax.axis_size("lon")
    n_lat = lax.axis_size("lat")
    nlon = width * n_lon
    nlat = rows * n_lat
    l = lax.axis_index("lat")
    hh = LAT_HALO
    hl = LON_HALO

    pairs = n_lon // 2
    same = [field] + [
        lax.ppermute(field, "lon", [(i, (i - 2 * k) % n_lon) for i in range(n_lon)])
        for k in range(1, pairs)
    ]
    sibling = [(i, i ^ 1) for i in range(n_lon)]
    first_sib = lax.ppermute(field, "lon", sibling)
    relay = lax.ppermute(jnp.concatenate(same[1:], axis=1), "lon", sibling)
    other = [first_sib] + jnp.split(relay, pairs - 1, axis=1)
    odd = (lax.axis_index("lon") % 2 == 1)
    blocks = []
    for k in range(pairs):
        blocks.append(jnp.where(odd, other[k], same[k]))
        blocks.append(jnp.where(odd, same[k], other[k]))
    full = jnp.concatenate(blocks, axis=1)

    w0 = width + 2 * hl
    span = w0 + 16
    amt = (offsets + hl + 8 - jnp.where(odd, width, 0)) % nlon
    nbits = (nlon - 1).bit_length()
    top = 1 << (nbits - 1)
    take = (amt // top % 2 == 1)[None, None, :]
    y = jnp.where(take, jnp.roll(full, top, axis=1), full)
    need = top - 1
    y = jnp.concatenate([y[:, nlon - need :], y[:, :span]], axis=1) if need else y[:, :span]
    for bit in range(nbits - 2, -1, -1):
        b = 1 << bit
        take = (amt // b % 2 == 1)[None, None, :]
        y = jnp.where(take, y[:, : y.shape[1] - b], y[:, b:])
    win = y

    s = fraction[None, None, :]
    w_one = -s * (s - 1.0) * (s - 2.0) / 6.0
    w_two = (s + 1.0) * (s - 1.0) * (s - 2.0) / 2.0
    w_three = -(s + 1.0) * s * (s - 2.0) / 2.0
    w_four = (s + 1.0) * s * (s - 1.0) / 6.0
    departure = (
        w_one * win[:, 9 : 9 + w0]
        + w_two * win[:, 8 : 8 + w0]
        + w_three * win[:, 7 : 7 + w0]
        + w_four * win[:, 6 : 6 + w0]
    )

    if n_lat == 2:
        sent = jnp.where(l == 0, departure[:, :, rows - hh :], departure[:, :, :hh])
        got = lax.ppermute(sent, "lat", [(0, 1), (1, 0)])
        halo = jnp.concatenate([got, got], axis=2)
    else:
        up = [(i, i + 1) for i in range(n_lat - 1)]
        down = [(i + 1, i) for i in range(n_lat - 1)]
        below = lax.ppermute(departure[:, :, rows - hh :], "lat", up)
        above = lax.ppermute(departure[:, :, :hh], "lat", down)
        halo = jnp.concatenate([above, below], axis=2)
    erows = rows + 2 * hh
    lane = jnp.arange(erows, dtype=jnp.int32)
    lat_rows = l * rows + jnp.where(lane < rows + hh, lane, lane - erows)
    valid = ((lat_rows >= 0) & (lat_rows < nlat)).astype(jnp.float32)[None, :]

    out = vcycle(
        helm, valid, departure.reshape(lev * w0, rows), halo.reshape(lev * w0, 2 * hh), w0, width, hl
    )
    return out.reshape(lev, width, rows)


def solution(mesh):
    return jax.shard_map(
        per_device,
        mesh=mesh,
        in_specs=(P(None, "lon", "lat"), P("lat"), P("lat"), P()),
        out_specs=P(None, "lon", "lat"),
        check_vma=False,
    )
```

```python
import functools

import jax
import jax.numpy as jnp
from jax import lax
from jax.experimental import pallas as pl
from jax.experimental.pallas import tpu as pltpu
from jax.sharding import PartitionSpec as P

SMOOTH = 2
COARSE = 4
OMEGA = 0.8


LAT_HALO = 64
LON_HALO = 32


def vcycle_kernel(helm_ref, rhs_ref, halo_ref, out_ref, *, wlon, width, hl, nlat):
    rows_total, rows = rhs_ref.shape
    b0 = jnp.concatenate([rhs_ref[...], halo_ref[...]], axis=1)
    cols = b0.shape[1]
    row = lax.broadcasted_iota(jnp.int32, (rows_total, cols), 0)
    col = lax.broadcasted_iota(jnp.int32, (rows_total, cols), 1)
    above = (cols - rows) // 2
    lat_rows = lax.axis_index("lat") * rows + jnp.where(col < rows + above, col, col - cols)
    valid = (lat_rows >= 0) & (lat_rows < nlat)
    coef0 = jnp.where(row < wlon, helm_ref[0], helm_ref[1])

    def shift(x, by, axis):
        n = x.shape[axis]
        return pltpu.roll(x, by % n, axis)

    def pair_sum(x, step):
        zonal = shift(x, step, 0) + shift(x, -step, 0)
        return zonal + shift(x, -step, 1) + shift(x, step, 1)

    def relax(x, rhs, coef, diag, gain, step):
        if x is None:
            x = rhs * gain
        else:
            applied = diag * x - coef * pair_sum(x, step)
            x = x + (rhs - applied) * gain
        return jnp.where(valid, x, 0.0)

    def defect(x, rhs, coef, diag, step):
        return rhs - (diag * x - coef * pair_sum(x, step))

    def restrict(x, step):
        lon_pair = x + shift(x, -step, 0)
        return (lon_pair + shift(lon_pair, -step, 1)) * 0.25

    def prolong(x, step):
        x = jnp.where(row % (2 * step) == step, shift(x, step, 0), x)
        return jnp.where(col % (2 * step) == step, shift(x, step, 1), x)

    coef1 = coef0 / 4.0
    coef2 = coef0 / 16.0
    diag0 = 1.0 + 4.0 * coef0
    diag1 = 1.0 + 4.0 * coef1
    diag2 = 1.0 + 4.0 * coef2
    gain0 = OMEGA / diag0
    gain1 = OMEGA / diag1
    gain2 = OMEGA / diag2

    x0 = None
    for sweep in range(SMOOTH):
        x0 = relax(x0, b0, coef0, diag0, gain0, 1)
    b1 = restrict(defect(x0, b0, coef0, diag0, 1), 1)
    x1 = None
    for sweep in range(SMOOTH):
        x1 = relax(x1, b1, coef1, diag1, gain1, 2)
    b2 = restrict(defect(x1, b1, coef1, diag1, 2), 2)
    x2 = None
    for sweep in range(COARSE):
        x2 = relax(x2, b2, coef2, diag2, gain2, 4)
    x1 = x1 + prolong(x2, 2)
    for sweep in range(SMOOTH):
        x1 = relax(x1, b1, coef1, diag1, gain1, 2)
    x0 = x0 + prolong(x1, 1)
    for sweep in range(SMOOTH):
        x0 = relax(x0, b0, coef0, diag0, gain0, 1)
    x0 = x0[:, :rows]
    for k in range(rows_total // wlon):
        out_ref[k * width : (k + 1) * width, :] = x0[k * wlon + hl : k * wlon + hl + width, :]


def vcycle(helm, rhs, halo, wlon, width, hl, nlat):
    lev = rhs.shape[0] // wlon
    return pl.pallas_call(
        functools.partial(vcycle_kernel, wlon=wlon, width=width, hl=hl, nlat=nlat),
        out_shape=jax.ShapeDtypeStruct((lev * width, rhs.shape[1]), rhs.dtype),
        in_specs=[
            pl.BlockSpec(memory_space=pltpu.SMEM),
            pl.BlockSpec(memory_space=pltpu.VMEM),
            pl.BlockSpec(memory_space=pltpu.VMEM),
        ],
        out_specs=pl.BlockSpec(memory_space=pltpu.VMEM),
        name="vcycle",
    )(helm, rhs, halo)


def per_device(field, offsets, fraction, helm):
    lev, width, rows = field.shape
    n_lon = lax.axis_size("lon")
    n_lat = lax.axis_size("lat")
    nlon = width * n_lon
    nlat = rows * n_lat
    l = lax.axis_index("lat")
    hh = LAT_HALO
    hl = LON_HALO

    pairs = n_lon // 2
    same = [field] + [
        lax.ppermute(field, "lon", [(i, (i - 2 * k) % n_lon) for i in range(n_lon)])
        for k in range(1, pairs)
    ]
    sibling = [(i, i ^ 1) for i in range(n_lon)]
    first_sib = lax.ppermute(field, "lon", sibling)
    relay = lax.ppermute(jnp.concatenate(same[1:], axis=1), "lon", sibling)
    other = [first_sib] + jnp.split(relay, pairs - 1, axis=1)
    odd = (lax.axis_index("lon") % 2 == 1)
    blocks = []
    for k in range(pairs):
        blocks.append(jnp.where(odd, other[k], same[k]))
        blocks.append(jnp.where(odd, same[k], other[k]))
    full = jnp.concatenate(blocks, axis=1)

    w0 = width + 2 * hl
    span = w0 + 16
    amt = (offsets + hl + 8 - jnp.where(odd, width, 0)) % nlon
    nbits = (nlon - 1).bit_length()
    top = 1 << (nbits - 1)
    take = (amt // top % 2 == 1)[None, None, :]
    y = jnp.where(take, jnp.roll(full, top, axis=1), full)
    need = top - 1
    y = jnp.concatenate([y[:, nlon - need :], y[:, :span]], axis=1) if need else y[:, :span]
    for bit in range(nbits - 2, -1, -1):
        b = 1 << bit
        take = (amt // b % 2 == 1)[None, None, :]
        y = jnp.where(take, y[:, : y.shape[1] - b], y[:, b:])
    win = y

    s = fraction[None, None, :]
    w_one = -s * (s - 1.0) * (s - 2.0) / 6.0
    w_two = (s + 1.0) * (s - 1.0) * (s - 2.0) / 2.0
    w_three = -(s + 1.0) * s * (s - 2.0) / 2.0
    w_four = (s + 1.0) * s * (s - 1.0) / 6.0
    departure = (
        w_one * win[:, 9 : 9 + w0]
        + w_two * win[:, 8 : 8 + w0]
        + w_three * win[:, 7 : 7 + w0]
        + w_four * win[:, 6 : 6 + w0]
    )

    if n_lat == 2:
        sent = jnp.where(l == 0, departure[:, :, rows - hh :], departure[:, :, :hh])
        halo = lax.ppermute(jnp.concatenate([sent, sent], axis=2), "lat", [(0, 1), (1, 0)])
    else:
        up = [(i, i + 1) for i in range(n_lat - 1)]
        down = [(i + 1, i) for i in range(n_lat - 1)]
        below = lax.ppermute(departure[:, :, rows - hh :], "lat", up)
        above = lax.ppermute(departure[:, :, :hh], "lat", down)
        halo = jnp.concatenate([above, below], axis=2)
    out = vcycle(
        helm, departure.reshape(lev * w0, rows), halo.reshape(lev * w0, 2 * hh), w0, width, hl, nlat
    )
    return out.reshape(lev, width, rows)


def solution(mesh):
    return jax.shard_map(
        per_device,
        mesh=mesh,
        in_specs=(P(None, "lon", "lat"), P("lat"), P("lat"), P()),
        out_specs=P(None, "lon", "lat"),
        check_vma=False,
    )
```

```python
import functools

import jax
import jax.numpy as jnp
from jax import lax
from jax.experimental import pallas as pl
from jax.experimental.pallas import tpu as pltpu
from jax.sharding import PartitionSpec as P

SMOOTH = 2
COARSE = 4
OMEGA = 0.8


LAT_HALO = 64
LON_HALO = 32


def vcycle_kernel(helm_ref, rhs_ref, halo_ref, out_ref, fine_ref, mid_ref, *, wlon, width, hl, nlat):
    rows_total, rows = rhs_ref.shape
    lev = rows_total // wlon
    b0 = jnp.concatenate([rhs_ref[...], halo_ref[...]], axis=1)
    cols = b0.shape[1]
    col = lax.broadcasted_iota(jnp.int32, (1, cols), 1)
    above = (cols - rows) // 2
    lat_rows = lax.axis_index("lat") * rows + jnp.where(col < rows + above, col, col - cols)
    valid = (lat_rows >= 0) & (lat_rows < nlat)

    def coef_of(n, scale):
        row = lax.broadcasted_iota(jnp.int32, (n, 1), 0)
        return jnp.where(row < n // lev, helm_ref[0], helm_ref[1]) / scale

    def shift(x, by, axis):
        n = x.shape[axis]
        return pltpu.roll(x, by % n, axis)

    def pair_sum(x, step):
        zonal = shift(x, 1, 0) + shift(x, -1, 0)
        return zonal + shift(x, -step, 1) + shift(x, step, 1)

    def relax(x, rhs, coef, diag, gain, step):
        if x is None:
            x = rhs * gain
        else:
            applied = diag * x - coef * pair_sum(x, step)
            x = x + (rhs - applied) * gain
        return jnp.where(valid, x, 0.0)

    def defect(x, rhs, coef, diag, step):
        return rhs - (diag * x - coef * pair_sum(x, step))

    tiles = range(cols // 128)

    def restrict(x, ref, step):
        n = x.shape[0] // 2
        for t in tiles:
            ref[t, : 2 * n, :] = x[:, t * 128 : (t + 1) * 128]
        lon_pair = jnp.concatenate(
            [ref[t, pl.ds(0, n, stride=2), :] + ref[t, pl.ds(1, n, stride=2), :] for t in tiles], axis=1
        )
        return (lon_pair + shift(lon_pair, -step, 1)) * 0.25

    def prolong(x, ref, step):
        n = x.shape[0]
        x = jnp.where(col % (2 * step) == step, shift(x, step, 1), x)
        for t in tiles:
            piece = x[:, t * 128 : (t + 1) * 128]
            ref[t, pl.ds(0, n, stride=2), :] = piece
            ref[t, pl.ds(1, n, stride=2), :] = piece
        return jnp.concatenate([ref[t, : 2 * n, :] for t in tiles], axis=1)

    n0 = rows_total
    coef0 = coef_of(n0, 1.0)
    coef1 = coef_of(n0 // 2, 4.0)
    coef2 = coef_of(n0 // 4, 16.0)
    diag0 = 1.0 + 4.0 * coef0
    diag1 = 1.0 + 4.0 * coef1
    diag2 = 1.0 + 4.0 * coef2
    gain0 = OMEGA / diag0
    gain1 = OMEGA / diag1
    gain2 = OMEGA / diag2

    x0 = None
    for sweep in range(SMOOTH):
        x0 = relax(x0, b0, coef0, diag0, gain0, 1)
    b1 = restrict(defect(x0, b0, coef0, diag0, 1), fine_ref, 1)
    x1 = None
    for sweep in range(SMOOTH):
        x1 = relax(x1, b1, coef1, diag1, gain1, 2)
    b2 = restrict(defect(x1, b1, coef1, diag1, 2), mid_ref, 2)
    x2 = None
    for sweep in range(COARSE):
        x2 = relax(x2, b2, coef2, diag2, gain2, 4)
    x1 = x1 + prolong(x2, mid_ref, 2)
    for sweep in range(SMOOTH):
        x1 = relax(x1, b1, coef1, diag1, gain1, 2)
    x0 = x0 + prolong(x1, fine_ref, 1)
    for sweep in range(SMOOTH):
        x0 = relax(x0, b0, coef0, diag0, gain0, 1)
    x0 = x0[:, :rows]
    for k in range(lev):
        out_ref[k * width : (k + 1) * width, :] = x0[k * wlon + hl : k * wlon + hl + width, :]


def vcycle(helm, rhs, halo, wlon, width, hl, nlat):
    lev = rhs.shape[0] // wlon
    return pl.pallas_call(
        functools.partial(vcycle_kernel, wlon=wlon, width=width, hl=hl, nlat=nlat),
        out_shape=jax.ShapeDtypeStruct((lev * width, rhs.shape[1]), rhs.dtype),
        in_specs=[
            pl.BlockSpec(memory_space=pltpu.SMEM),
            pl.BlockSpec(memory_space=pltpu.VMEM),
            pl.BlockSpec(memory_space=pltpu.VMEM),
        ],
        out_specs=pl.BlockSpec(memory_space=pltpu.VMEM),
        scratch_shapes=[
            pltpu.VMEM(((rhs.shape[1] + halo.shape[1]) // 128, rhs.shape[0], 128), jnp.float32),
            pltpu.VMEM(((rhs.shape[1] + halo.shape[1]) // 128, rhs.shape[0] // 2, 128), jnp.float32),
        ],
        name="vcycle",
    )(helm, rhs, halo)


def per_device(field, offsets, fraction, helm):
    lev, width, rows = field.shape
    n_lon = lax.axis_size("lon")
    n_lat = lax.axis_size("lat")
    nlon = width * n_lon
    nlat = rows * n_lat
    l = lax.axis_index("lat")
    hh = LAT_HALO
    hl = LON_HALO

    pairs = n_lon // 2
    same = [field] + [
        lax.ppermute(field, "lon", [(i, (i - 2 * k) % n_lon) for i in range(n_lon)])
        for k in range(1, pairs)
    ]
    sibling = [(i, i ^ 1) for i in range(n_lon)]
    first_sib = lax.ppermute(field, "lon", sibling)
    relay = lax.ppermute(jnp.concatenate(same[1:], axis=1), "lon", sibling)
    other = [first_sib] + jnp.split(relay, pairs - 1, axis=1)
    odd = (lax.axis_index("lon") % 2 == 1)
    blocks = []
    for k in range(pairs):
        blocks.append(jnp.where(odd, other[k], same[k]))
        blocks.append(jnp.where(odd, same[k], other[k]))
    full = jnp.concatenate(blocks, axis=1)

    w0 = width + 2 * hl
    span = w0 + 16
    amt = (offsets + hl + 8 - jnp.where(odd, width, 0)) % nlon
    nbits = (nlon - 1).bit_length()
    top = 1 << (nbits - 1)
    take = (amt // top % 2 == 1)[None, None, :]
    y = jnp.where(take, jnp.roll(full, top, axis=1), full)
    need = top - 1
    y = jnp.concatenate([y[:, nlon - need :], y[:, :span]], axis=1) if need else y[:, :span]
    for bit in range(nbits - 2, -1, -1):
        b = 1 << bit
        take = (amt // b % 2 == 1)[None, None, :]
        y = jnp.where(take, y[:, : y.shape[1] - b], y[:, b:])
    win = y

    s = fraction[None, None, :]
    w_one = -s * (s - 1.0) * (s - 2.0) / 6.0
    w_two = (s + 1.0) * (s - 1.0) * (s - 2.0) / 2.0
    w_three = -(s + 1.0) * s * (s - 2.0) / 2.0
    w_four = (s + 1.0) * s * (s - 1.0) / 6.0
    departure = (
        w_one * win[:, 9 : 9 + w0]
        + w_two * win[:, 8 : 8 + w0]
        + w_three * win[:, 7 : 7 + w0]
        + w_four * win[:, 6 : 6 + w0]
    )

    if n_lat == 2:
        sent = jnp.where(l == 0, departure[:, :, rows - hh :], departure[:, :, :hh])
        halo = lax.ppermute(jnp.concatenate([sent, sent], axis=2), "lat", [(0, 1), (1, 0)])
    else:
        up = [(i, i + 1) for i in range(n_lat - 1)]
        down = [(i + 1, i) for i in range(n_lat - 1)]
        below = lax.ppermute(departure[:, :, rows - hh :], "lat", up)
        above = lax.ppermute(departure[:, :, :hh], "lat", down)
        halo = jnp.concatenate([above, below], axis=2)
    out = vcycle(
        helm, departure.reshape(lev * w0, rows), halo.reshape(lev * w0, 2 * hh), w0, width, hl, nlat
    )
    return out.reshape(lev, width, rows)


def solution(mesh):
    return jax.shard_map(
        per_device,
        mesh=mesh,
        in_specs=(P(None, "lon", "lat"), P("lat"), P("lat"), P()),
        out_specs=P(None, "lon", "lat"),
        check_vma=False,
    )
```

```python
import functools

import jax
import jax.numpy as jnp
from jax import lax
from jax.experimental import pallas as pl
from jax.experimental.pallas import tpu as pltpu
from jax.sharding import PartitionSpec as P

SMOOTH = 2
COARSE = 4
OMEGA = 0.8


LAT_HALO = 64
LON_HALO = 32


def vcycle_kernel(helm_ref, rhs_ref, halo_ref, out_ref, fine_ref, mid_ref, lat_ref, *, wlon, width, hl, nlat):
    rows_total, rows = rhs_ref.shape
    lev = rows_total // wlon
    cols = lat_ref.shape[1]
    lat_ref[:, :rows] = rhs_ref[...]
    if halo_ref.shape[1] == cols - rows:
        lat_ref[:, rows:] = halo_ref[...]
    else:
        above = halo_ref.shape[1]
        lat_ref[:, rows : rows + above] = halo_ref[...]
        lat_ref[:, rows + above :] = halo_ref[...]
    b0 = lat_ref[...]
    col = lax.broadcasted_iota(jnp.int32, (1, cols), 1)
    above = (cols - rows) // 2
    lat_rows = lax.axis_index("lat") * rows + jnp.where(col < rows + above, col, col - cols)
    valid = (lat_rows >= 0) & (lat_rows < nlat)

    def coef_of(n, scale):
        row = lax.broadcasted_iota(jnp.int32, (n, 1), 0)
        return jnp.where(row < n // lev, helm_ref[0], helm_ref[1]) / scale

    def shift(x, by, axis):
        n = x.shape[axis]
        return pltpu.roll(x, by % n, axis)

    def pair_sum(x, step):
        zonal = shift(x, 1, 0) + shift(x, -1, 0)
        return zonal + shift(x, -step, 1) + shift(x, step, 1)

    def relax(x, rhs, coef, diag, gain, step):
        if x is None:
            x = rhs * gain
        else:
            applied = diag * x - coef * pair_sum(x, step)
            x = x + (rhs - applied) * gain
        return jnp.where(valid, x, 0.0)

    def defect(x, rhs, coef, diag, step):
        return rhs - (diag * x - coef * pair_sum(x, step))

    tiles = range(cols // 128)

    def restrict(x, ref, step):
        n = x.shape[0] // 2
        for t in tiles:
            ref[t, : 2 * n, :] = x[:, t * 128 : (t + 1) * 128]
        lon_pair = jnp.concatenate(
            [ref[t, pl.ds(0, n, stride=2), :] + ref[t, pl.ds(1, n, stride=2), :] for t in tiles], axis=1
        )
        return (lon_pair + shift(lon_pair, -step, 1)) * 0.25

    def prolong(x, ref, step):
        n = x.shape[0]
        x = jnp.where(col % (2 * step) == step, shift(x, step, 1), x)
        for t in tiles:
            piece = x[:, t * 128 : (t + 1) * 128]
            ref[t, pl.ds(0, n, stride=2), :] = piece
            ref[t, pl.ds(1, n, stride=2), :] = piece
        return jnp.concatenate([ref[t, : 2 * n, :] for t in tiles], axis=1)

    n0 = rows_total
    coef0 = coef_of(n0, 1.0)
    coef1 = coef_of(n0 // 2, 4.0)
    coef2 = coef_of(n0 // 4, 16.0)
    diag0 = 1.0 + 4.0 * coef0
    diag1 = 1.0 + 4.0 * coef1
    diag2 = 1.0 + 4.0 * coef2
    gain0 = OMEGA / diag0
    gain1 = OMEGA / diag1
    gain2 = OMEGA / diag2

    x0 = None
    for sweep in range(SMOOTH):
        x0 = relax(x0, b0, coef0, diag0, gain0, 1)
    b1 = restrict(defect(x0, b0, coef0, diag0, 1), fine_ref, 1)
    x1 = None
    for sweep in range(SMOOTH):
        x1 = relax(x1, b1, coef1, diag1, gain1, 2)
    b2 = restrict(defect(x1, b1, coef1, diag1, 2), mid_ref, 2)
    x2 = None
    for sweep in range(COARSE):
        x2 = relax(x2, b2, coef2, diag2, gain2, 4)
    x1 = x1 + prolong(x2, mid_ref, 2)
    for sweep in range(SMOOTH):
        x1 = relax(x1, b1, coef1, diag1, gain1, 2)
    x0 = x0 + prolong(x1, fine_ref, 1)
    for sweep in range(SMOOTH):
        x0 = relax(x0, b0, coef0, diag0, gain0, 1)
    x0 = x0[:, :rows]
    for k in range(lev):
        out_ref[k * width : (k + 1) * width, :] = x0[k * wlon + hl : k * wlon + hl + width, :]


def vcycle(helm, rhs, halo, cols, wlon, width, hl, nlat):
    lev = rhs.shape[0] // wlon
    return pl.pallas_call(
        functools.partial(vcycle_kernel, wlon=wlon, width=width, hl=hl, nlat=nlat),
        out_shape=jax.ShapeDtypeStruct((lev * width, rhs.shape[1]), rhs.dtype),
        in_specs=[
            pl.BlockSpec(memory_space=pltpu.SMEM),
            pl.BlockSpec(memory_space=pltpu.VMEM),
            pl.BlockSpec(memory_space=pltpu.VMEM),
        ],
        out_specs=pl.BlockSpec(memory_space=pltpu.VMEM),
        scratch_shapes=[
            pltpu.VMEM((cols // 128, rhs.shape[0], 128), jnp.float32),
            pltpu.VMEM((cols // 128, rhs.shape[0] // 2, 128), jnp.float32),
            pltpu.VMEM((rhs.shape[0], cols), jnp.float32),
        ],
        name="vcycle",
    )(helm, rhs, halo)


def per_device(field, offsets, fraction, helm):
    lev, width, rows = field.shape
    n_lon = lax.axis_size("lon")
    n_lat = lax.axis_size("lat")
    nlon = width * n_lon
    nlat = rows * n_lat
    l = lax.axis_index("lat")
    hh = LAT_HALO
    hl = LON_HALO

    pairs = n_lon // 2
    same = [field] + [
        lax.ppermute(field, "lon", [(i, (i - 2 * k) % n_lon) for i in range(n_lon)])
        for k in range(1, pairs)
    ]
    sibling = [(i, i ^ 1) for i in range(n_lon)]
    first_sib = lax.ppermute(field, "lon", sibling)
    relay = lax.ppermute(jnp.concatenate(same[1:], axis=1), "lon", sibling)
    other = [first_sib] + jnp.split(relay, pairs - 1, axis=1)
    odd = (lax.axis_index("lon") % 2 == 1)
    blocks = []
    for k in range(pairs):
        blocks.append(jnp.where(odd, other[k], same[k]))
        blocks.append(jnp.where(odd, same[k], other[k]))
    full = jnp.concatenate(blocks, axis=1)

    w0 = width + 2 * hl
    span = w0 + 16
    amt = (offsets + hl + 8 - jnp.where(odd, width, 0)) % nlon
    nbits = (nlon - 1).bit_length()
    top = 1 << (nbits - 1)
    take = (amt // top % 2 == 1)[None, None, :]
    y = jnp.where(take, jnp.roll(full, top, axis=1), full)
    need = top - 1
    y = jnp.concatenate([y[:, nlon - need :], y[:, :span]], axis=1) if need else y[:, :span]
    for bit in range(nbits - 2, -1, -1):
        b = 1 << bit
        take = (amt // b % 2 == 1)[None, None, :]
        y = jnp.where(take, y[:, : y.shape[1] - b], y[:, b:])
    win = y

    s = fraction[None, None, :]
    w_one = -s * (s - 1.0) * (s - 2.0) / 6.0
    w_two = (s + 1.0) * (s - 1.0) * (s - 2.0) / 2.0
    w_three = -(s + 1.0) * s * (s - 2.0) / 2.0
    w_four = (s + 1.0) * s * (s - 1.0) / 6.0
    departure = (
        w_one * win[:, 9 : 9 + w0]
        + w_two * win[:, 8 : 8 + w0]
        + w_three * win[:, 7 : 7 + w0]
        + w_four * win[:, 6 : 6 + w0]
    )

    if n_lat == 2:
        sent = jnp.where(l == 0, departure[:, :, rows - hh :], departure[:, :, :hh])
        halo = lax.ppermute(sent, "lat", [(0, 1), (1, 0)])
    else:
        up = [(i, i + 1) for i in range(n_lat - 1)]
        down = [(i + 1, i) for i in range(n_lat - 1)]
        below = lax.ppermute(departure[:, :, rows - hh :], "lat", up)
        above = lax.ppermute(departure[:, :, :hh], "lat", down)
        halo = jnp.concatenate([above, below], axis=2)
    out = vcycle(
        helm,
        departure.reshape(lev * w0, rows),
        halo.reshape(lev * w0, halo.shape[2]),
        rows + 2 * hh,
        w0,
        width,
        hl,
        nlat,
    )
    return out.reshape(lev, width, rows)


def solution(mesh):
    return jax.shard_map(
        per_device,
        mesh=mesh,
        in_specs=(P(None, "lon", "lat"), P("lat"), P("lat"), P()),
        out_specs=P(None, "lon", "lat"),
        check_vma=False,
    )
```

```python
import functools

import jax
import jax.numpy as jnp
from jax import lax
from jax.experimental import pallas as pl
from jax.experimental.pallas import tpu as pltpu
from jax.sharding import PartitionSpec as P

SMOOTH = 2
COARSE = 4
OMEGA = 0.8


LAT_HALO = 64
LON_HALO = 32


def vcycle_kernel(*refs, wlon, width, hl, nlat, with_halo, masked):
    if with_halo:
        helm_ref, rhs_ref, halo_ref, out_ref, fine_ref, mid_ref, lat_ref = refs
    else:
        helm_ref, rhs_ref, out_ref, fine_ref, mid_ref, lat_ref = refs
    rows_total, rows = rhs_ref.shape
    lev = rows_total // wlon
    cols = lat_ref.shape[1]
    lat_ref[:, :rows] = rhs_ref[...]
    if not with_halo:
        if cols > rows:
            lat_ref[:, rows:] = jnp.zeros((rows_total, cols - rows), jnp.float32)
    elif halo_ref.shape[1] == cols - rows:
        lat_ref[:, rows:] = halo_ref[...]
    else:
        above = halo_ref.shape[1]
        lat_ref[:, rows : rows + above] = halo_ref[...]
        lat_ref[:, rows + above :] = halo_ref[...]
    b0 = lat_ref[...]
    col = lax.broadcasted_iota(jnp.int32, (1, cols), 1)
    above = (cols - rows) // 2
    lat_rows = lax.axis_index("lat") * rows + jnp.where(col < rows + above, col, col - cols)
    valid = (lat_rows >= 0) & (lat_rows < nlat) if masked else None

    def coef_of(n, scale):
        row = lax.broadcasted_iota(jnp.int32, (n, 1), 0)
        return jnp.where(row < n // lev, helm_ref[0], helm_ref[1]) / scale

    def shift(x, by, axis):
        n = x.shape[axis]
        return pltpu.roll(x, by % n, axis)

    def pair_sum(x, step):
        zonal = shift(x, 1, 0) + shift(x, -1, 0)
        return zonal + shift(x, -step, 1) + shift(x, step, 1)

    def relax(x, rhs, coef, diag, gain, step):
        if x is None:
            x = rhs * gain
        else:
            applied = diag * x - coef * pair_sum(x, step)
            x = x + (rhs - applied) * gain
        return x if valid is None else jnp.where(valid, x, 0.0)

    def defect(x, rhs, coef, diag, step):
        return rhs - (diag * x - coef * pair_sum(x, step))

    tiles = range(cols // 128)

    def restrict(x, ref, step):
        n = x.shape[0] // 2
        for t in tiles:
            ref[t, : 2 * n, :] = x[:, t * 128 : (t + 1) * 128]
        lon_pair = jnp.concatenate(
            [ref[t, pl.ds(0, n, stride=2), :] + ref[t, pl.ds(1, n, stride=2), :] for t in tiles], axis=1
        )
        return (lon_pair + shift(lon_pair, -step, 1)) * 0.25

    def prolong(x, ref, step):
        n = x.shape[0]
        x = jnp.where(col % (2 * step) == step, shift(x, step, 1), x)
        for t in tiles:
            piece = x[:, t * 128 : (t + 1) * 128]
            ref[t, pl.ds(0, n, stride=2), :] = piece
            ref[t, pl.ds(1, n, stride=2), :] = piece
        return jnp.concatenate([ref[t, : 2 * n, :] for t in tiles], axis=1)

    n0 = rows_total
    coef0 = coef_of(n0, 1.0)
    coef1 = coef_of(n0 // 2, 4.0)
    coef2 = coef_of(n0 // 4, 16.0)
    diag0 = 1.0 + 4.0 * coef0
    diag1 = 1.0 + 4.0 * coef1
    diag2 = 1.0 + 4.0 * coef2
    gain0 = OMEGA / diag0
    gain1 = OMEGA / diag1
    gain2 = OMEGA / diag2

    x0 = None
    for sweep in range(SMOOTH):
        x0 = relax(x0, b0, coef0, diag0, gain0, 1)
    b1 = restrict(defect(x0, b0, coef0, diag0, 1), fine_ref, 1)
    x1 = None
    for sweep in range(SMOOTH):
        x1 = relax(x1, b1, coef1, diag1, gain1, 2)
    b2 = restrict(defect(x1, b1, coef1, diag1, 2), mid_ref, 2)
    x2 = None
    for sweep in range(COARSE):
        x2 = relax(x2, b2, coef2, diag2, gain2, 4)
    x1 = x1 + prolong(x2, mid_ref, 2)
    for sweep in range(SMOOTH):
        x1 = relax(x1, b1, coef1, diag1, gain1, 2)
    x0 = x0 + prolong(x1, fine_ref, 1)
    for sweep in range(SMOOTH):
        x0 = relax(x0, b0, coef0, diag0, gain0, 1)
    x0 = x0[:, :rows]
    for k in range(lev):
        out_ref[k * width : (k + 1) * width, :] = x0[k * wlon + hl : k * wlon + hl + width, :]


def vcycle(helm, rhs, halo, cols, wlon, width, hl, nlat, masked=True):
    lev = rhs.shape[0] // wlon
    operands = (helm, rhs) if halo is None else (helm, rhs, halo)
    return pl.pallas_call(
        functools.partial(
            vcycle_kernel,
            wlon=wlon,
            width=width,
            hl=hl,
            nlat=nlat,
            with_halo=halo is not None,
            masked=masked,
        ),
        out_shape=jax.ShapeDtypeStruct((lev * width, rhs.shape[1]), rhs.dtype),
        in_specs=[pl.BlockSpec(memory_space=pltpu.SMEM)]
        + [pl.BlockSpec(memory_space=pltpu.VMEM)] * (len(operands) - 1),
        out_specs=pl.BlockSpec(memory_space=pltpu.VMEM),
        scratch_shapes=[
            pltpu.VMEM((cols // 128, rhs.shape[0], 128), jnp.float32),
            pltpu.VMEM((cols // 128, rhs.shape[0] // 2, 128), jnp.float32),
            pltpu.VMEM((rhs.shape[0], cols), jnp.float32),
        ],
        name="vcycle",
    )(*operands)


def per_device(field, offsets, fraction, helm):
    lev, width, rows = field.shape
    n_lon = lax.axis_size("lon")
    n_lat = lax.axis_size("lat")
    nlon = width * n_lon
    nlat = rows * n_lat
    l = lax.axis_index("lat")
    hh = LAT_HALO
    hl = LON_HALO

    pairs = n_lon // 2
    same = [field] + [
        lax.ppermute(field, "lon", [(i, (i - 2 * k) % n_lon) for i in range(n_lon)])
        for k in range(1, pairs)
    ]
    sibling = [(i, i ^ 1) for i in range(n_lon)]
    first_sib = lax.ppermute(field, "lon", sibling)
    relay = lax.ppermute(jnp.concatenate(same[1:], axis=1), "lon", sibling)
    other = [first_sib] + jnp.split(relay, pairs - 1, axis=1)
    odd = (lax.axis_index("lon") % 2 == 1)
    blocks = []
    for k in range(pairs):
        blocks.append(jnp.where(odd, other[k], same[k]))
        blocks.append(jnp.where(odd, same[k], other[k]))
    full = jnp.concatenate(blocks, axis=1)

    w0 = width + 2 * hl
    span = w0 + 16
    amt = (offsets + hl + 8 - jnp.where(odd, width, 0)) % nlon
    nbits = (nlon - 1).bit_length()
    top = 1 << (nbits - 1)
    take = (amt // top % 2 == 1)[None, None, :]
    y = jnp.where(take, jnp.roll(full, top, axis=1), full)
    need = top - 1
    y = jnp.concatenate([y[:, nlon - need :], y[:, :span]], axis=1) if need else y[:, :span]
    for bit in range(nbits - 2, -1, -1):
        b = 1 << bit
        take = (amt // b % 2 == 1)[None, None, :]
        y = jnp.where(take, y[:, : y.shape[1] - b], y[:, b:])
    win = y

    s = fraction[None, None, :]
    w_one = -s * (s - 1.0) * (s - 2.0) / 6.0
    w_two = (s + 1.0) * (s - 1.0) * (s - 2.0) / 2.0
    w_three = -(s + 1.0) * s * (s - 2.0) / 2.0
    w_four = (s + 1.0) * s * (s - 1.0) / 6.0
    departure = (
        w_one * win[:, 9 : 9 + w0]
        + w_two * win[:, 8 : 8 + w0]
        + w_three * win[:, 7 : 7 + w0]
        + w_four * win[:, 6 : 6 + w0]
    )

    cols = rows + 2 * hh
    if n_lat == 2:
        sent = jnp.where(l == 0, departure[:, :, rows - hh :], departure[:, :, :hh])
        halo = lax.ppermute(sent, "lat", [(0, 1), (1, 0)])
        band = vcycle(helm, departure.reshape(lev * w0, rows), None, cols, w0, width, hl, nlat)
        across = jnp.where(
            l == 0,
            jnp.concatenate([sent, halo], axis=2),
            jnp.concatenate([halo, sent], axis=2),
        )
        edge = vcycle(
            helm, across.reshape(lev * w0, 2 * hh), None, 2 * hh, w0, width, hl, nlat, masked=False
        )
        near = hh // 2
        out = jnp.where(
            l == 0,
            jnp.concatenate([band[:, : rows - near], edge[:, near:hh]], axis=1),
            jnp.concatenate([edge[:, hh : hh + near], band[:, near:]], axis=1),
        )
        return out.reshape(lev, width, rows)
    up = [(i, i + 1) for i in range(n_lat - 1)]
    down = [(i + 1, i) for i in range(n_lat - 1)]
    below = lax.ppermute(departure[:, :, rows - hh :], "lat", up)
    above = lax.ppermute(departure[:, :, :hh], "lat", down)
    halo = jnp.concatenate([above, below], axis=2)
    out = vcycle(
        helm,
        departure.reshape(lev * w0, rows),
        halo.reshape(lev * w0, 2 * hh),
        cols,
        w0,
        width,
        hl,
        nlat,
    )
    return out.reshape(lev, width, rows)


def solution(mesh):
    return jax.shard_map(
        per_device,
        mesh=mesh,
        in_specs=(P(None, "lon", "lat"), P("lat"), P("lat"), P()),
        out_specs=P(None, "lon", "lat"),
        check_vma=False,
    )
```

```python
import functools

import jax
import jax.numpy as jnp
from jax import lax
from jax.experimental import pallas as pl
from jax.experimental.pallas import tpu as pltpu
from jax.sharding import PartitionSpec as P

SMOOTH = 2
COARSE = 4
OMEGA = 0.8


LAT_HALO = 64
LON_HALO = 32


def vcycle_kernel(helm_ref, rhs_ref, halo_ref, out_ref, fine_ref, mid_ref, lat_ref, *, wlon, width, hl, nlat):
    rows_total, rows = rhs_ref.shape
    lev = rows_total // wlon
    cols = lat_ref.shape[1]
    lat_ref[:, :rows] = rhs_ref[...]
    if halo_ref.shape[1] == cols - rows:
        lat_ref[:, rows:] = halo_ref[...]
    else:
        above = halo_ref.shape[1]
        lat_ref[:, rows : rows + above] = halo_ref[...]
        lat_ref[:, rows + above :] = halo_ref[...]
    b0 = lat_ref[...]
    col = lax.broadcasted_iota(jnp.int32, (1, cols), 1)
    above = (cols - rows) // 2
    lat_rows = lax.axis_index("lat") * rows + jnp.where(col < rows + above, col, col - cols)
    valid = (lat_rows >= 0) & (lat_rows < nlat)

    def coef_of(n, scale):
        row = lax.broadcasted_iota(jnp.int32, (n, 1), 0)
        return jnp.where(row < n // lev, helm_ref[0], helm_ref[1]) / scale

    def shift(x, by, axis):
        n = x.shape[axis]
        return pltpu.roll(x, by % n, axis)

    def pair_sum(x, step):
        zonal = shift(x, 1, 0) + shift(x, -1, 0)
        return zonal + shift(x, -step, 1) + shift(x, step, 1)

    def relax(x, rhs, coef, diag, gain, step):
        if x is None:
            x = rhs * gain
        else:
            applied = diag * x - coef * pair_sum(x, step)
            x = x + (rhs - applied) * gain
        return jnp.where(valid, x, 0.0)

    def defect(x, rhs, coef, diag, step):
        return rhs - (diag * x - coef * pair_sum(x, step))

    tiles = range(cols // 128)

    def restrict(x, ref, step):
        n = x.shape[0] // 2
        for t in tiles:
            ref[t, : 2 * n, :] = x[:, t * 128 : (t + 1) * 128]
        lon_pair = jnp.concatenate(
            [ref[t, pl.ds(0, n, stride=2), :] + ref[t, pl.ds(1, n, stride=2), :] for t in tiles], axis=1
        )
        return (lon_pair + shift(lon_pair, -step, 1)) * 0.25

    def prolong(x, ref, step):
        n = x.shape[0]
        x = jnp.where(col % (2 * step) == step, shift(x, step, 1), x)
        for t in tiles:
            piece = x[:, t * 128 : (t + 1) * 128]
            ref[t, pl.ds(0, n, stride=2), :] = piece
            ref[t, pl.ds(1, n, stride=2), :] = piece
        return jnp.concatenate([ref[t, : 2 * n, :] for t in tiles], axis=1)

    n0 = rows_total
    coef0 = coef_of(n0, 1.0)
    coef1 = coef_of(n0 // 2, 4.0)
    coef2 = coef_of(n0 // 4, 16.0)
    diag0 = 1.0 + 4.0 * coef0
    diag1 = 1.0 + 4.0 * coef1
    diag2 = 1.0 + 4.0 * coef2
    gain0 = OMEGA / diag0
    gain1 = OMEGA / diag1
    gain2 = OMEGA / diag2

    x0 = None
    for sweep in range(SMOOTH):
        x0 = relax(x0, b0, coef0, diag0, gain0, 1)
    b1 = restrict(defect(x0, b0, coef0, diag0, 1), fine_ref, 1)
    x1 = None
    for sweep in range(SMOOTH):
        x1 = relax(x1, b1, coef1, diag1, gain1, 2)
    b2 = restrict(defect(x1, b1, coef1, diag1, 2), mid_ref, 2)
    x2 = None
    for sweep in range(COARSE):
        x2 = relax(x2, b2, coef2, diag2, gain2, 4)
    x1 = x1 + prolong(x2, mid_ref, 2)
    for sweep in range(SMOOTH):
        x1 = relax(x1, b1, coef1, diag1, gain1, 2)
    x0 = x0 + prolong(x1, fine_ref, 1)
    for sweep in range(SMOOTH):
        x0 = relax(x0, b0, coef0, diag0, gain0, 1)
    x0 = x0[:, :rows]
    for k in range(lev):
        out_ref[k * width : (k + 1) * width, :] = x0[k * wlon + hl : k * wlon + hl + width, :]


def vcycle(helm, rhs, halo, cols, wlon, width, hl, nlat):
    lev = rhs.shape[0] // wlon
    return pl.pallas_call(
        functools.partial(vcycle_kernel, wlon=wlon, width=width, hl=hl, nlat=nlat),
        out_shape=jax.ShapeDtypeStruct((lev * width, rhs.shape[1]), rhs.dtype),
        in_specs=[
            pl.BlockSpec(memory_space=pltpu.SMEM),
            pl.BlockSpec(memory_space=pltpu.VMEM),
            pl.BlockSpec(memory_space=pltpu.VMEM),
        ],
        out_specs=pl.BlockSpec(memory_space=pltpu.VMEM),
        scratch_shapes=[
            pltpu.VMEM((cols // 128, rhs.shape[0], 128), jnp.float32),
            pltpu.VMEM((cols // 128, rhs.shape[0] // 2, 128), jnp.float32),
            pltpu.VMEM((rhs.shape[0], cols), jnp.float32),
        ],
        name="vcycle",
    )(helm, rhs, halo)


def per_device(field, offsets, fraction, helm):
    lev, width, rows = field.shape
    n_lon = lax.axis_size("lon")
    n_lat = lax.axis_size("lat")
    nlon = width * n_lon
    nlat = rows * n_lat
    l = lax.axis_index("lat")
    hh = LAT_HALO
    hl = LON_HALO

    pairs = n_lon // 2
    same = [field] + [
        lax.ppermute(field, "lon", [(i, (i - 2 * k) % n_lon) for i in range(n_lon)])
        for k in range(1, pairs)
    ]
    sibling = [(i, i ^ 1) for i in range(n_lon)]
    relay = lax.ppermute(jnp.concatenate(same, axis=1), "lon", sibling)
    other = jnp.split(relay, pairs, axis=1)
    odd = (lax.axis_index("lon") % 2 == 1)
    blocks = []
    for k in range(pairs):
        blocks.append(jnp.where(odd, other[k], same[k]))
        blocks.append(jnp.where(odd, same[k], other[k]))
    full = jnp.concatenate(blocks, axis=1)

    w0 = width + 2 * hl
    span = w0 + 16
    amt = (offsets + hl + 8 - jnp.where(odd, width, 0)) % nlon
    nbits = (nlon - 1).bit_length()
    top = 1 << (nbits - 1)
    take = (amt // top % 2 == 1)[None, None, :]
    y = jnp.where(take, jnp.roll(full, top, axis=1), full)
    need = top - 1
    y = jnp.concatenate([y[:, nlon - need :], y[:, :span]], axis=1) if need else y[:, :span]
    for bit in range(nbits - 2, -1, -1):
        b = 1 << bit
        take = (amt // b % 2 == 1)[None, None, :]
        y = jnp.where(take, y[:, : y.shape[1] - b], y[:, b:])
    win = y

    s = fraction[None, None, :]
    w_one = -s * (s - 1.0) * (s - 2.0) / 6.0
    w_two = (s + 1.0) * (s - 1.0) * (s - 2.0) / 2.0
    w_three = -(s + 1.0) * s * (s - 2.0) / 2.0
    w_four = (s + 1.0) * s * (s - 1.0) / 6.0
    departure = (
        w_one * win[:, 9 : 9 + w0]
        + w_two * win[:, 8 : 8 + w0]
        + w_three * win[:, 7 : 7 + w0]
        + w_four * win[:, 6 : 6 + w0]
    )

    if n_lat == 2:
        sent = jnp.where(l == 0, departure[:, :, rows - hh :], departure[:, :, :hh])
        halo = lax.ppermute(sent, "lat", [(0, 1), (1, 0)])
    else:
        up = [(i, i + 1) for i in range(n_lat - 1)]
        down = [(i + 1, i) for i in range(n_lat - 1)]
        below = lax.ppermute(departure[:, :, rows - hh :], "lat", up)
        above = lax.ppermute(departure[:, :, :hh], "lat", down)
        halo = jnp.concatenate([above, below], axis=2)
    out = vcycle(
        helm,
        departure.reshape(lev * w0, rows),
        halo.reshape(lev * w0, halo.shape[2]),
        rows + 2 * hh,
        w0,
        width,
        hl,
        nlat,
    )
    return out.reshape(lev, width, rows)


def solution(mesh):
    return jax.shard_map(
        per_device,
        mesh=mesh,
        in_specs=(P(None, "lon", "lat"), P("lat"), P("lat"), P()),
        out_specs=P(None, "lon", "lat"),
        check_vma=False,
    )
```

```python
import functools

import jax
import jax.numpy as jnp
from jax import lax
from jax.experimental import pallas as pl
from jax.experimental.pallas import tpu as pltpu
from jax.sharding import PartitionSpec as P

SMOOTH = 2
COARSE = 4
OMEGA = 0.8


LAT_HALO = 64
LON_HALO = 32


def vcycle_kernel(helm_ref, rhs_ref, halo_ref, out_ref, fine_ref, mid_ref, lat_ref, *, wlon, width, hl, nlat):
    rows_total, rows = rhs_ref.shape
    lev = rows_total // wlon
    cols = lat_ref.shape[1]
    lat_ref[:, :rows] = rhs_ref[...]
    if halo_ref.shape[1] == cols - rows:
        lat_ref[:, rows:] = halo_ref[...]
    else:
        above = halo_ref.shape[1]
        lat_ref[:, rows : rows + above] = halo_ref[...]
        lat_ref[:, rows + above :] = halo_ref[...]
    b0 = lat_ref[...]
    col = lax.broadcasted_iota(jnp.int32, (1, cols), 1)
    above = (cols - rows) // 2
    lat_rows = lax.axis_index("lat") * rows + jnp.where(col < rows + above, col, col - cols)
    valid = (lat_rows >= 0) & (lat_rows < nlat)

    def coef_of(n, scale):
        row = lax.broadcasted_iota(jnp.int32, (n, 1), 0)
        return jnp.where(row < n // lev, helm_ref[0], helm_ref[1]) / scale

    def shift(x, by, axis):
        n = x.shape[axis]
        return pltpu.roll(x, by % n, axis)

    def pair_sum(x, step):
        zonal = shift(x, 1, 0) + shift(x, -1, 0)
        return zonal + shift(x, -step, 1) + shift(x, step, 1)

    def relax(x, rhs, coef, diag, gain, step):
        if x is None:
            x = rhs * gain
        else:
            applied = diag * x - coef * pair_sum(x, step)
            x = x + (rhs - applied) * gain
        return jnp.where(valid, x, 0.0)

    def defect(x, rhs, coef, diag, step):
        return rhs - (diag * x - coef * pair_sum(x, step))

    tiles = range(cols // 128)

    def restrict(x, ref, step):
        n = x.shape[0] // 2
        for t in tiles:
            ref[t, : 2 * n, :] = x[:, t * 128 : (t + 1) * 128]
        lon_pair = jnp.concatenate(
            [ref[t, pl.ds(0, n, stride=2), :] + ref[t, pl.ds(1, n, stride=2), :] for t in tiles], axis=1
        )
        return (lon_pair + shift(lon_pair, -step, 1)) * 0.25

    def prolong(x, ref, step):
        n = x.shape[0]
        x = jnp.where(col % (2 * step) == step, shift(x, step, 1), x)
        for t in tiles:
            piece = x[:, t * 128 : (t + 1) * 128]
            ref[t, pl.ds(0, n, stride=2), :] = piece
            ref[t, pl.ds(1, n, stride=2), :] = piece
        return jnp.concatenate([ref[t, : 2 * n, :] for t in tiles], axis=1)

    n0 = rows_total
    coef0 = coef_of(n0, 1.0)
    coef1 = coef_of(n0 // 2, 4.0)
    coef2 = coef_of(n0 // 4, 16.0)
    diag0 = 1.0 + 4.0 * coef0
    diag1 = 1.0 + 4.0 * coef1
    diag2 = 1.0 + 4.0 * coef2
    gain0 = OMEGA / diag0
    gain1 = OMEGA / diag1
    gain2 = OMEGA / diag2

    x0 = None
    for sweep in range(SMOOTH):
        x0 = relax(x0, b0, coef0, diag0, gain0, 1)
    b1 = restrict(defect(x0, b0, coef0, diag0, 1), fine_ref, 1)
    x1 = None
    for sweep in range(SMOOTH):
        x1 = relax(x1, b1, coef1, diag1, gain1, 2)
    b2 = restrict(defect(x1, b1, coef1, diag1, 2), mid_ref, 2)
    x2 = None
    for sweep in range(COARSE):
        x2 = relax(x2, b2, coef2, diag2, gain2, 4)
    x1 = x1 + prolong(x2, mid_ref, 2)
    for sweep in range(SMOOTH):
        x1 = relax(x1, b1, coef1, diag1, gain1, 2)
    x0 = x0 + prolong(x1, fine_ref, 1)
    for sweep in range(SMOOTH):
        x0 = relax(x0, b0, coef0, diag0, gain0, 1)
    x0 = x0[:, :rows]
    for k in range(lev):
        out_ref[k * width : (k + 1) * width, :] = x0[k * wlon + hl : k * wlon + hl + width, :]


def vcycle(helm, rhs, halo, cols, wlon, width, hl, nlat):
    lev = rhs.shape[0] // wlon
    return pl.pallas_call(
        functools.partial(vcycle_kernel, wlon=wlon, width=width, hl=hl, nlat=nlat),
        out_shape=jax.ShapeDtypeStruct((lev * width, rhs.shape[1]), rhs.dtype),
        in_specs=[
            pl.BlockSpec(memory_space=pltpu.SMEM),
            pl.BlockSpec(memory_space=pltpu.VMEM),
            pl.BlockSpec(memory_space=pltpu.VMEM),
        ],
        out_specs=pl.BlockSpec(memory_space=pltpu.VMEM),
        scratch_shapes=[
            pltpu.VMEM((cols // 128, rhs.shape[0], 128), jnp.float32),
            pltpu.VMEM((cols // 128, rhs.shape[0] // 2, 128), jnp.float32),
            pltpu.VMEM((rhs.shape[0], cols), jnp.float32),
        ],
        name="vcycle",
    )(helm, rhs, halo)


def per_device(field, offsets, fraction, helm):
    lev, width, rows = field.shape
    n_lon = lax.axis_size("lon")
    n_lat = lax.axis_size("lat")
    nlon = width * n_lon
    nlat = rows * n_lat
    l = lax.axis_index("lat")
    hh = LAT_HALO
    hl = LON_HALO

    pairs = n_lon // 2
    same = [field] + [
        lax.ppermute(field, "lon", [(i, (i - 2 * k) % n_lon) for i in range(n_lon)])
        for k in range(1, pairs)
    ]
    sibling = [(i, i ^ 1) for i in range(n_lon)]
    relay = lax.ppermute(jnp.concatenate(same, axis=1), "lon", sibling)
    other = jnp.split(relay, pairs, axis=1)
    odd = (lax.axis_index("lon") % 2 == 1)
    blocks = []
    for k in range(pairs):
        blocks.append(jnp.where(odd, other[k], same[k]))
        blocks.append(jnp.where(odd, same[k], other[k]))
    full = jnp.concatenate(blocks, axis=1)

    w0 = width + 2 * hl
    span = w0 + 16

    def departure_of(full, offsets, fraction):
        amt = (offsets + hl + 8 - jnp.where(odd, width, 0)) % nlon
        nbits = (nlon - 1).bit_length()
        top = 1 << (nbits - 1)
        take = (amt // top % 2 == 1)[None, None, :]
        y = jnp.where(take, jnp.roll(full, top, axis=1), full)
        need = top - 1
        y = jnp.concatenate([y[:, nlon - need :], y[:, :span]], axis=1) if need else y[:, :span]
        for bit in range(nbits - 2, -1, -1):
            b = 1 << bit
            take = (amt // b % 2 == 1)[None, None, :]
            y = jnp.where(take, y[:, : y.shape[1] - b], y[:, b:])
        win = y
        s = fraction[None, None, :]
        w_one = -s * (s - 1.0) * (s - 2.0) / 6.0
        w_two = (s + 1.0) * (s - 1.0) * (s - 2.0) / 2.0
        w_three = -(s + 1.0) * s * (s - 2.0) / 2.0
        w_four = (s + 1.0) * s * (s - 1.0) / 6.0
        return (
            w_one * win[:, 9 : 9 + w0]
            + w_two * win[:, 8 : 8 + w0]
            + w_three * win[:, 7 : 7 + w0]
            + w_four * win[:, 6 : 6 + w0]
        )

    if n_lat == 2:
        def edge(x):
            return jnp.where(l == 0, x[..., rows - hh :], x[..., :hh])

        sent = departure_of(edge(full), edge(offsets), edge(fraction))
        halo = lax.ppermute(sent, "lat", [(0, 1), (1, 0)])
        departure = departure_of(full, offsets, fraction)
    else:
        departure = departure_of(full, offsets, fraction)
        up = [(i, i + 1) for i in range(n_lat - 1)]
        down = [(i + 1, i) for i in range(n_lat - 1)]
        below = lax.ppermute(departure[:, :, rows - hh :], "lat", up)
        above = lax.ppermute(departure[:, :, :hh], "lat", down)
        halo = jnp.concatenate([above, below], axis=2)
    out = vcycle(
        helm,
        departure.reshape(lev * w0, rows),
        halo.reshape(lev * w0, halo.shape[2]),
        rows + 2 * hh,
        w0,
        width,
        hl,
        nlat,
    )
    return out.reshape(lev, width, rows)


def solution(mesh):
    return jax.shard_map(
        per_device,
        mesh=mesh,
        in_specs=(P(None, "lon", "lat"), P("lat"), P("lat"), P()),
        out_specs=P(None, "lon", "lat"),
        check_vma=False,
    )
```

```python
import functools

import jax
import jax.numpy as jnp
from jax import lax
from jax.experimental import pallas as pl
from jax.experimental.pallas import tpu as pltpu
from jax.sharding import PartitionSpec as P

SMOOTH = 2
COARSE = 4
OMEGA = 0.8


LAT_HALO = 64
LON_HALO = 32


def vcycle_kernel(helm_ref, rhs_ref, halo_ref, out_ref, fine_ref, mid_ref, lat_ref, *, wlon, width, hl, nlat):
    rows_total, rows = rhs_ref.shape
    lev = rows_total // wlon
    cols = lat_ref.shape[1]
    lat_ref[:, :rows] = rhs_ref[...]
    if halo_ref.shape[1] == cols - rows:
        lat_ref[:, rows:] = halo_ref[...]
    else:
        above = halo_ref.shape[1]
        lat_ref[:, rows : rows + above] = halo_ref[...]
        lat_ref[:, rows + above :] = halo_ref[...]
    b0 = lat_ref[...]
    col = lax.broadcasted_iota(jnp.int32, (1, cols), 1)
    above = (cols - rows) // 2
    lat_rows = lax.axis_index("lat") * rows + jnp.where(col < rows + above, col, col - cols)
    valid = (lat_rows >= 0) & (lat_rows < nlat)

    def coef_of(n, scale):
        row = lax.broadcasted_iota(jnp.int32, (n, 1), 0)
        return jnp.where(row < n // lev, helm_ref[0], helm_ref[1]) / scale

    def shift(x, by, axis):
        n = x.shape[axis]
        return pltpu.roll(x, by % n, axis)

    def pair_sum(x, step):
        zonal = shift(x, 1, 0) + shift(x, -1, 0)
        return zonal + shift(x, -step, 1) + shift(x, step, 1)

    def relax(x, rhs, coef, diag, gain, step):
        if x is None:
            return rhs * gain
        applied = diag * x - coef * pair_sum(x, step)
        return x + (rhs - applied) * gain

    def defect(x, rhs, coef, diag, step):
        return rhs - (diag * x - coef * pair_sum(x, step))

    tiles = range(cols // 128)

    def restrict(x, ref, step):
        n = x.shape[0] // 2
        for t in tiles:
            ref[t, : 2 * n, :] = x[:, t * 128 : (t + 1) * 128]
        lon_pair = jnp.concatenate(
            [ref[t, pl.ds(0, n, stride=2), :] + ref[t, pl.ds(1, n, stride=2), :] for t in tiles], axis=1
        )
        return (lon_pair + shift(lon_pair, -step, 1)) * 0.25

    def prolong(x, ref, step):
        n = x.shape[0]
        x = jnp.where(col % (2 * step) == step, shift(x, step, 1), x)
        for t in tiles:
            piece = x[:, t * 128 : (t + 1) * 128]
            ref[t, pl.ds(0, n, stride=2), :] = piece
            ref[t, pl.ds(1, n, stride=2), :] = piece
        return jnp.concatenate([ref[t, : 2 * n, :] for t in tiles], axis=1)

    n0 = rows_total
    coef0 = coef_of(n0, 1.0)
    coef1 = coef_of(n0 // 2, 4.0)
    coef2 = coef_of(n0 // 4, 16.0)
    diag0 = 1.0 + 4.0 * coef0
    diag1 = 1.0 + 4.0 * coef1
    diag2 = 1.0 + 4.0 * coef2
    gain0 = jnp.where(valid, OMEGA / diag0, 0.0)
    gain1 = jnp.where(valid, OMEGA / diag1, 0.0)
    gain2 = jnp.where(valid, OMEGA / diag2, 0.0)

    x0 = None
    for sweep in range(SMOOTH):
        x0 = relax(x0, b0, coef0, diag0, gain0, 1)
    b1 = restrict(defect(x0, b0, coef0, diag0, 1), fine_ref, 1)
    x1 = None
    for sweep in range(SMOOTH):
        x1 = relax(x1, b1, coef1, diag1, gain1, 2)
    b2 = restrict(defect(x1, b1, coef1, diag1, 2), mid_ref, 2)
    x2 = None
    for sweep in range(COARSE):
        x2 = relax(x2, b2, coef2, diag2, gain2, 4)
    x1 = x1 + prolong(x2, mid_ref, 2)
    for sweep in range(SMOOTH):
        x1 = relax(x1, b1, coef1, diag1, gain1, 2)
    x0 = x0 + prolong(x1, fine_ref, 1)
    for sweep in range(SMOOTH):
        x0 = relax(x0, b0, coef0, diag0, gain0, 1)
    x0 = x0[:, :rows]
    for k in range(lev):
        out_ref[k * width : (k + 1) * width, :] = x0[k * wlon + hl : k * wlon + hl + width, :]


def vcycle(helm, rhs, halo, cols, wlon, width, hl, nlat):
    lev = rhs.shape[0] // wlon
    return pl.pallas_call(
        functools.partial(vcycle_kernel, wlon=wlon, width=width, hl=hl, nlat=nlat),
        out_shape=jax.ShapeDtypeStruct((lev * width, rhs.shape[1]), rhs.dtype),
        in_specs=[
            pl.BlockSpec(memory_space=pltpu.SMEM),
            pl.BlockSpec(memory_space=pltpu.VMEM),
            pl.BlockSpec(memory_space=pltpu.VMEM),
        ],
        out_specs=pl.BlockSpec(memory_space=pltpu.VMEM),
        scratch_shapes=[
            pltpu.VMEM((cols // 128, rhs.shape[0], 128), jnp.float32),
            pltpu.VMEM((cols // 128, rhs.shape[0] // 2, 128), jnp.float32),
            pltpu.VMEM((rhs.shape[0], cols), jnp.float32),
        ],
        name="vcycle",
    )(helm, rhs, halo)


def per_device(field, offsets, fraction, helm):
    lev, width, rows = field.shape
    n_lon = lax.axis_size("lon")
    n_lat = lax.axis_size("lat")
    nlon = width * n_lon
    nlat = rows * n_lat
    l = lax.axis_index("lat")
    hh = LAT_HALO
    hl = LON_HALO

    pairs = n_lon // 2
    same = [field] + [
        lax.ppermute(field, "lon", [(i, (i - 2 * k) % n_lon) for i in range(n_lon)])
        for k in range(1, pairs)
    ]
    sibling = [(i, i ^ 1) for i in range(n_lon)]
    relay = lax.ppermute(jnp.concatenate(same, axis=1), "lon", sibling)
    other = jnp.split(relay, pairs, axis=1)
    odd = (lax.axis_index("lon") % 2 == 1)
    blocks = []
    for k in range(pairs):
        blocks.append(jnp.where(odd, other[k], same[k]))
        blocks.append(jnp.where(odd, same[k], other[k]))
    full = jnp.concatenate(blocks, axis=1)

    w0 = width + 2 * hl
    span = w0 + 16
    amt = (offsets + hl + 8 - jnp.where(odd, width, 0)) % nlon
    nbits = (nlon - 1).bit_length()
    top = 1 << (nbits - 1)
    take = (amt // top % 2 == 1)[None, None, :]
    y = jnp.where(take, jnp.roll(full, top, axis=1), full)
    need = top - 1
    y = jnp.concatenate([y[:, nlon - need :], y[:, :span]], axis=1) if need else y[:, :span]
    for bit in range(nbits - 2, -1, -1):
        b = 1 << bit
        take = (amt // b % 2 == 1)[None, None, :]
        y = jnp.where(take, y[:, : y.shape[1] - b], y[:, b:])
    win = y

    s = fraction[None, None, :]
    w_one = -s * (s - 1.0) * (s - 2.0) / 6.0
    w_two = (s + 1.0) * (s - 1.0) * (s - 2.0) / 2.0
    w_three = -(s + 1.0) * s * (s - 2.0) / 2.0
    w_four = (s + 1.0) * s * (s - 1.0) / 6.0
    departure = (
        w_one * win[:, 9 : 9 + w0]
        + w_two * win[:, 8 : 8 + w0]
        + w_three * win[:, 7 : 7 + w0]
        + w_four * win[:, 6 : 6 + w0]
    )

    if n_lat == 2:
        sent = jnp.where(l == 0, departure[:, :, rows - hh :], departure[:, :, :hh])
        halo = lax.ppermute(sent, "lat", [(0, 1), (1, 0)])
    else:
        up = [(i, i + 1) for i in range(n_lat - 1)]
        down = [(i + 1, i) for i in range(n_lat - 1)]
        below = lax.ppermute(departure[:, :, rows - hh :], "lat", up)
        above = lax.ppermute(departure[:, :, :hh], "lat", down)
        halo = jnp.concatenate([above, below], axis=2)
    out = vcycle(
        helm,
        departure.reshape(lev * w0, rows),
        halo.reshape(lev * w0, halo.shape[2]),
        rows + 2 * hh,
        w0,
        width,
        hl,
        nlat,
    )
    return out.reshape(lev, width, rows)


def solution(mesh):
    return jax.shard_map(
        per_device,
        mesh=mesh,
        in_specs=(P(None, "lon", "lat"), P("lat"), P("lat"), P()),
        out_specs=P(None, "lon", "lat"),
        check_vma=False,
    )
```

```python
import functools

import jax
import jax.numpy as jnp
from jax import lax
from jax.experimental import pallas as pl
from jax.experimental.pallas import tpu as pltpu
from jax.sharding import PartitionSpec as P

SMOOTH = 2
COARSE = 4
OMEGA = 0.8


LAT_HALO = 64
LON_HALO = 32


def vcycle_kernel(helm_ref, rhs_ref, halo_ref, out_ref, fine_ref, mid_ref, lat_ref, *, wlon, width, hl, nlat):
    rows_total, rows = rhs_ref.shape
    lev = rows_total // wlon
    cols = lat_ref.shape[1]
    lat_ref[:, :rows] = rhs_ref[...]
    if halo_ref.shape[1] == cols - rows:
        lat_ref[:, rows:] = halo_ref[...]
    else:
        above = halo_ref.shape[1]
        lat_ref[:, rows : rows + above] = halo_ref[...]
        lat_ref[:, rows + above :] = halo_ref[...]
    b0 = lat_ref[...]
    col = lax.broadcasted_iota(jnp.int32, (1, cols), 1)
    above = (cols - rows) // 2
    lat_rows = lax.axis_index("lat") * rows + jnp.where(col < rows + above, col, col - cols)
    valid = (lat_rows >= 0) & (lat_rows < nlat)

    def coef_of(n, scale):
        row = lax.broadcasted_iota(jnp.int32, (n, 1), 0)
        return jnp.where(row < n // lev, helm_ref[0], helm_ref[1]) / scale

    def shift(x, by, axis):
        n = x.shape[axis]
        return pltpu.roll(x, by % n, axis)

    def pair_sum(x, step):
        zonal = shift(x, 1, 0) + shift(x, -1, 0)
        return zonal + shift(x, -step, 1) + shift(x, step, 1)

    def relax(x, rhs_gain, keep, coef_gain, step):
        if x is None:
            return rhs_gain
        return x * keep + rhs_gain + pair_sum(x, step) * coef_gain

    def defect(x, rhs, coef, diag, step):
        return rhs - (diag * x - coef * pair_sum(x, step))

    tiles = range(cols // 128)

    def restrict(x, ref, step):
        n = x.shape[0] // 2
        for t in tiles:
            ref[t, : 2 * n, :] = x[:, t * 128 : (t + 1) * 128]
        lon_pair = jnp.concatenate(
            [ref[t, pl.ds(0, n, stride=2), :] + ref[t, pl.ds(1, n, stride=2), :] for t in tiles], axis=1
        )
        return (lon_pair + shift(lon_pair, -step, 1)) * 0.25

    def prolong(x, ref, step):
        n = x.shape[0]
        x = jnp.where(col % (2 * step) == step, shift(x, step, 1), x)
        for t in tiles:
            piece = x[:, t * 128 : (t + 1) * 128]
            ref[t, pl.ds(0, n, stride=2), :] = piece
            ref[t, pl.ds(1, n, stride=2), :] = piece
        return jnp.concatenate([ref[t, : 2 * n, :] for t in tiles], axis=1)

    n0 = rows_total
    coef0 = coef_of(n0, 1.0)
    coef1 = coef_of(n0 // 2, 4.0)
    coef2 = coef_of(n0 // 4, 16.0)
    diag0 = 1.0 + 4.0 * coef0
    diag1 = 1.0 + 4.0 * coef1
    diag2 = 1.0 + 4.0 * coef2
    gain0 = jnp.where(valid, OMEGA / diag0, 0.0)
    gain1 = jnp.where(valid, OMEGA / diag1, 0.0)
    gain2 = jnp.where(valid, OMEGA / diag2, 0.0)

    keep0, keep1, keep2 = 1.0 - diag0 * gain0, 1.0 - diag1 * gain1, 1.0 - diag2 * gain2
    cg0, cg1, cg2 = coef0 * gain0, coef1 * gain1, coef2 * gain2

    x0 = None
    bg0 = b0 * gain0
    for sweep in range(SMOOTH):
        x0 = relax(x0, bg0, keep0, cg0, 1)
    b1 = restrict(defect(x0, b0, coef0, diag0, 1), fine_ref, 1)
    x1 = None
    bg1 = b1 * gain1
    for sweep in range(SMOOTH):
        x1 = relax(x1, bg1, keep1, cg1, 2)
    b2 = restrict(defect(x1, b1, coef1, diag1, 2), mid_ref, 2)
    x2 = None
    bg2 = b2 * gain2
    for sweep in range(COARSE):
        x2 = relax(x2, bg2, keep2, cg2, 4)
    x1 = x1 + prolong(x2, mid_ref, 2)
    for sweep in range(SMOOTH):
        x1 = relax(x1, bg1, keep1, cg1, 2)
    x0 = x0 + prolong(x1, fine_ref, 1)
    for sweep in range(SMOOTH):
        x0 = relax(x0, bg0, keep0, cg0, 1)
    x0 = x0[:, :rows]
    for k in range(lev):
        out_ref[k * width : (k + 1) * width, :] = x0[k * wlon + hl : k * wlon + hl + width, :]


def vcycle(helm, rhs, halo, cols, wlon, width, hl, nlat):
    lev = rhs.shape[0] // wlon
    return pl.pallas_call(
        functools.partial(vcycle_kernel, wlon=wlon, width=width, hl=hl, nlat=nlat),
        out_shape=jax.ShapeDtypeStruct((lev * width, rhs.shape[1]), rhs.dtype),
        in_specs=[
            pl.BlockSpec(memory_space=pltpu.SMEM),
            pl.BlockSpec(memory_space=pltpu.VMEM),
            pl.BlockSpec(memory_space=pltpu.VMEM),
        ],
        out_specs=pl.BlockSpec(memory_space=pltpu.VMEM),
        scratch_shapes=[
            pltpu.VMEM((cols // 128, rhs.shape[0], 128), jnp.float32),
            pltpu.VMEM((cols // 128, rhs.shape[0] // 2, 128), jnp.float32),
            pltpu.VMEM((rhs.shape[0], cols), jnp.float32),
        ],
        name="vcycle",
    )(helm, rhs, halo)


def per_device(field, offsets, fraction, helm):
    lev, width, rows = field.shape
    n_lon = lax.axis_size("lon")
    n_lat = lax.axis_size("lat")
    nlon = width * n_lon
    nlat = rows * n_lat
    l = lax.axis_index("lat")
    hh = LAT_HALO
    hl = LON_HALO

    pairs = n_lon // 2
    same = [field] + [
        lax.ppermute(field, "lon", [(i, (i - 2 * k) % n_lon) for i in range(n_lon)])
        for k in range(1, pairs)
    ]
    sibling = [(i, i ^ 1) for i in range(n_lon)]
    relay = lax.ppermute(jnp.concatenate(same, axis=1), "lon", sibling)
    other = jnp.split(relay, pairs, axis=1)
    odd = (lax.axis_index("lon") % 2 == 1)
    blocks = []
    for k in range(pairs):
        blocks.append(jnp.where(odd, other[k], same[k]))
        blocks.append(jnp.where(odd, same[k], other[k]))
    full = jnp.concatenate(blocks, axis=1)

    w0 = width + 2 * hl
    span = w0 + 16
    amt = (offsets + hl + 8 - jnp.where(odd, width, 0)) % nlon
    nbits = (nlon - 1).bit_length()
    top = 1 << (nbits - 1)
    take = (amt // top % 2 == 1)[None, None, :]
    y = jnp.where(take, jnp.roll(full, top, axis=1), full)
    need = top - 1
    y = jnp.concatenate([y[:, nlon - need :], y[:, :span]], axis=1) if need else y[:, :span]
    for bit in range(nbits - 2, -1, -1):
        b = 1 << bit
        take = (amt // b % 2 == 1)[None, None, :]
        y = jnp.where(take, y[:, : y.shape[1] - b], y[:, b:])
    win = y

    s = fraction[None, None, :]
    w_one = -s * (s - 1.0) * (s - 2.0) / 6.0
    w_two = (s + 1.0) * (s - 1.0) * (s - 2.0) / 2.0
    w_three = -(s + 1.0) * s * (s - 2.0) / 2.0
    w_four = (s + 1.0) * s * (s - 1.0) / 6.0
    departure = (
        w_one * win[:, 9 : 9 + w0]
        + w_two * win[:, 8 : 8 + w0]
        + w_three * win[:, 7 : 7 + w0]
        + w_four * win[:, 6 : 6 + w0]
    )

    if n_lat == 2:
        sent = jnp.where(l == 0, departure[:, :, rows - hh :], departure[:, :, :hh])
        halo = lax.ppermute(sent, "lat", [(0, 1), (1, 0)])
    else:
        up = [(i, i + 1) for i in range(n_lat - 1)]
        down = [(i + 1, i) for i in range(n_lat - 1)]
        below = lax.ppermute(departure[:, :, rows - hh :], "lat", up)
        above = lax.ppermute(departure[:, :, :hh], "lat", down)
        halo = jnp.concatenate([above, below], axis=2)
    out = vcycle(
        helm,
        departure.reshape(lev * w0, rows),
        halo.reshape(lev * w0, halo.shape[2]),
        rows + 2 * hh,
        w0,
        width,
        hl,
        nlat,
    )
    return out.reshape(lev, width, rows)


def solution(mesh):
    return jax.shard_map(
        per_device,
        mesh=mesh,
        in_specs=(P(None, "lon", "lat"), P("lat"), P("lat"), P()),
        out_specs=P(None, "lon", "lat"),
        check_vma=False,
    )
```

```python
import functools

import jax
import jax.numpy as jnp
from jax import lax
from jax.experimental import pallas as pl
from jax.experimental.pallas import tpu as pltpu
from jax.sharding import PartitionSpec as P

SMOOTH = 2
COARSE = 4
OMEGA = 0.8


LAT_HALO = 64
LON_HALO = 32


def vcycle_kernel(helm_ref, rhs_ref, halo_ref, out_ref, fine_ref, mid_ref, lat_ref, *, wlon, width, hl, nlat):
    rows_total, rows = rhs_ref.shape
    lev = rows_total // wlon
    cols = lat_ref.shape[1]
    halo = halo_ref[...]
    if halo.shape[1] < cols - rows:
        halo = jnp.concatenate([halo, halo], axis=1)
    b0 = jnp.concatenate([rhs_ref[...], halo], axis=1)
    col = lax.broadcasted_iota(jnp.int32, (1, cols), 1)
    above = (cols - rows) // 2
    lat_rows = lax.axis_index("lat") * rows + jnp.where(col < rows + above, col, col - cols)
    valid = (lat_rows >= 0) & (lat_rows < nlat)

    def coef_of(n, scale):
        row = lax.broadcasted_iota(jnp.int32, (n, 1), 0)
        return jnp.where(row < n // lev, helm_ref[0], helm_ref[1]) / scale

    def shift(x, by, axis):
        n = x.shape[axis]
        return pltpu.roll(x, by % n, axis)

    def pair_sum(x, step):
        zonal = shift(x, 1, 0) + shift(x, -1, 0)
        return zonal + shift(x, -step, 1) + shift(x, step, 1)

    def relax(x, rhs, coef, diag, gain, step):
        if x is None:
            return rhs * gain
        applied = diag * x - coef * pair_sum(x, step)
        return x + (rhs - applied) * gain

    def defect(x, rhs, coef, diag, step):
        return rhs - (diag * x - coef * pair_sum(x, step))

    tiles = range(cols // 128)

    def restrict(x, ref, step):
        n = x.shape[0] // 2
        for t in tiles:
            ref[t, : 2 * n, :] = x[:, t * 128 : (t + 1) * 128]
        lon_pair = jnp.concatenate(
            [ref[t, pl.ds(0, n, stride=2), :] + ref[t, pl.ds(1, n, stride=2), :] for t in tiles], axis=1
        )
        return (lon_pair + shift(lon_pair, -step, 1)) * 0.25

    def prolong(x, ref, step):
        n = x.shape[0]
        x = jnp.where(col % (2 * step) == step, shift(x, step, 1), x)
        for t in tiles:
            piece = x[:, t * 128 : (t + 1) * 128]
            ref[t, pl.ds(0, n, stride=2), :] = piece
            ref[t, pl.ds(1, n, stride=2), :] = piece
        return jnp.concatenate([ref[t, : 2 * n, :] for t in tiles], axis=1)

    n0 = rows_total
    coef0 = coef_of(n0, 1.0)
    coef1 = coef_of(n0 // 2, 4.0)
    coef2 = coef_of(n0 // 4, 16.0)
    diag0 = 1.0 + 4.0 * coef0
    diag1 = 1.0 + 4.0 * coef1
    diag2 = 1.0 + 4.0 * coef2
    gain0 = jnp.where(valid, OMEGA / diag0, 0.0)
    gain1 = jnp.where(valid, OMEGA / diag1, 0.0)
    gain2 = jnp.where(valid, OMEGA / diag2, 0.0)

    x0 = None
    for sweep in range(SMOOTH):
        x0 = relax(x0, b0, coef0, diag0, gain0, 1)
    b1 = restrict(defect(x0, b0, coef0, diag0, 1), fine_ref, 1)
    x1 = None
    for sweep in range(SMOOTH):
        x1 = relax(x1, b1, coef1, diag1, gain1, 2)
    b2 = restrict(defect(x1, b1, coef1, diag1, 2), mid_ref, 2)
    x2 = None
    for sweep in range(COARSE):
        x2 = relax(x2, b2, coef2, diag2, gain2, 4)
    x1 = x1 + prolong(x2, mid_ref, 2)
    for sweep in range(SMOOTH):
        x1 = relax(x1, b1, coef1, diag1, gain1, 2)
    x0 = x0 + prolong(x1, fine_ref, 1)
    for sweep in range(SMOOTH):
        x0 = relax(x0, b0, coef0, diag0, gain0, 1)
    x0 = x0[:, :rows]
    for k in range(lev):
        out_ref[k * width : (k + 1) * width, :] = x0[k * wlon + hl : k * wlon + hl + width, :]


def vcycle(helm, rhs, halo, cols, wlon, width, hl, nlat):
    lev = rhs.shape[0] // wlon
    return pl.pallas_call(
        functools.partial(vcycle_kernel, wlon=wlon, width=width, hl=hl, nlat=nlat),
        out_shape=jax.ShapeDtypeStruct((lev * width, rhs.shape[1]), rhs.dtype),
        in_specs=[
            pl.BlockSpec(memory_space=pltpu.SMEM),
            pl.BlockSpec(memory_space=pltpu.VMEM),
            pl.BlockSpec(memory_space=pltpu.VMEM),
        ],
        out_specs=pl.BlockSpec(memory_space=pltpu.VMEM),
        scratch_shapes=[
            pltpu.VMEM((cols // 128, rhs.shape[0], 128), jnp.float32),
            pltpu.VMEM((cols // 128, rhs.shape[0] // 2, 128), jnp.float32),
            pltpu.VMEM((rhs.shape[0], cols), jnp.float32),
        ],
        name="vcycle",
    )(helm, rhs, halo)


def per_device(field, offsets, fraction, helm):
    lev, width, rows = field.shape
    n_lon = lax.axis_size("lon")
    n_lat = lax.axis_size("lat")
    nlon = width * n_lon
    nlat = rows * n_lat
    l = lax.axis_index("lat")
    hh = LAT_HALO
    hl = LON_HALO

    pairs = n_lon // 2
    same = [field] + [
        lax.ppermute(field, "lon", [(i, (i - 2 * k) % n_lon) for i in range(n_lon)])
        for k in range(1, pairs)
    ]
    sibling = [(i, i ^ 1) for i in range(n_lon)]
    relay = lax.ppermute(jnp.concatenate(same, axis=1), "lon", sibling)
    other = jnp.split(relay, pairs, axis=1)
    odd = (lax.axis_index("lon") % 2 == 1)
    blocks = []
    for k in range(pairs):
        blocks.append(jnp.where(odd, other[k], same[k]))
        blocks.append(jnp.where(odd, same[k], other[k]))
    full = jnp.concatenate(blocks, axis=1)

    w0 = width + 2 * hl
    span = w0 + 16
    amt = (offsets + hl + 8 - jnp.where(odd, width, 0)) % nlon
    nbits = (nlon - 1).bit_length()
    top = 1 << (nbits - 1)
    take = (amt // top % 2 == 1)[None, None, :]
    y = jnp.where(take, jnp.roll(full, top, axis=1), full)
    need = top - 1
    y = jnp.concatenate([y[:, nlon - need :], y[:, :span]], axis=1) if need else y[:, :span]
    for bit in range(nbits - 2, -1, -1):
        b = 1 << bit
        take = (amt // b % 2 == 1)[None, None, :]
        y = jnp.where(take, y[:, : y.shape[1] - b], y[:, b:])
    win = y

    s = fraction[None, None, :]
    w_one = -s * (s - 1.0) * (s - 2.0) / 6.0
    w_two = (s + 1.0) * (s - 1.0) * (s - 2.0) / 2.0
    w_three = -(s + 1.0) * s * (s - 2.0) / 2.0
    w_four = (s + 1.0) * s * (s - 1.0) / 6.0
    departure = (
        w_one * win[:, 9 : 9 + w0]
        + w_two * win[:, 8 : 8 + w0]
        + w_three * win[:, 7 : 7 + w0]
        + w_four * win[:, 6 : 6 + w0]
    )

    if n_lat == 2:
        sent = jnp.where(l == 0, departure[:, :, rows - hh :], departure[:, :, :hh])
        halo = lax.ppermute(sent, "lat", [(0, 1), (1, 0)])
    else:
        up = [(i, i + 1) for i in range(n_lat - 1)]
        down = [(i + 1, i) for i in range(n_lat - 1)]
        below = lax.ppermute(departure[:, :, rows - hh :], "lat", up)
        above = lax.ppermute(departure[:, :, :hh], "lat", down)
        halo = jnp.concatenate([above, below], axis=2)
    out = vcycle(
        helm,
        departure.reshape(lev * w0, rows),
        halo.reshape(lev * w0, halo.shape[2]),
        rows + 2 * hh,
        w0,
        width,
        hl,
        nlat,
    )
    return out.reshape(lev, width, rows)


def solution(mesh):
    return jax.shard_map(
        per_device,
        mesh=mesh,
        in_specs=(P(None, "lon", "lat"), P("lat"), P("lat"), P()),
        out_specs=P(None, "lon", "lat"),
        check_vma=False,
    )
```
